32 devices in a mesh: dom: 8 (over z, x), grp: 4 (over y, core).
Axes of the slice: x: 2, y: 2, z: 4, core: 2. Of those that a mesh axis runs over, the one named last changes fastest.
Arguments:
- x_current: bfloat16 [131072, 128], P(('dom', 'grp')), may hold values from -6 to 6
- x_cached: bfloat16 [131072, 128], P(('dom', 'grp')), may hold values from -6 to 6
- w_self: bfloat16 [128, 512], replicated, may hold values from -0.5 to 0.5
- w_neigh: bfloat16 [128, 512], replicated, may hold values from -1 to 1
- bias: float32 [512], replicated, may hold values from -3 to 3
- tile_columns: int32 [1024, 40], P(('dom', 'grp')), may hold values from 0 to 159
- tile_count: int32 [1024], P(('dom', 'grp')), may hold values from 1 to 40, as said below
- adjacency: int32 [1024, 40, 2048], P(('dom', 'grp')), may hold values from 0 to 255, as said below
- degree: int32 [131072], P(('dom', 'grp')), may hold values from 1 to 5128, as said below
- boundary_blocks: int32 [32, 1], P(('dom', 'grp')), may hold values from 0 to 31
Outputs:
- hidden: bfloat16 [131072, 512], P(('dom', 'grp'))
The draws below stay inside these ranges and needn't reach their ends.
Inputs may be any that keep to these rules, and one draw needn't show every extreme that they name: `tile_count`: every device has a row block with all 40 slots live. `adjacency`: 8 entries of a tile row packed into each word, bit b for column 8 c + b. `degree`: at least the number of ones in the row of the live tiles of the node's row block.
All inputs are finite; a program needn't handle non-finite values.
Results may differ from the reference program's by a relative error of at most 0.0025.
Values may be sent and summed in bfloat16 or wider, within the bound.
No kernel may reach another device: no remote copies, remote signals or barrier semaphores. Data moves between devices by JAX's collectives and lax.ppermute only.
A program may use at most 192 MiB of HBM per device.

```python
import jax
import jax.numpy as jnp
from jax import lax

F = 128
H = 512
TILE = 128
TPR = 40
BB = 1
NODES = 131072
DBLK = 32
PBLK = 128
ROWBLOCKS = 1024
N_DOM = 8
N_GRP = 4


def count_bits(words):
    value = words - (lax.shift_right_logical(words, 1) & 1431655765)
    value = (value & 858993459) + (lax.shift_right_logical(value, 2) & 858993459)
    value = value + lax.shift_right_logical(value, 4) & 252645135
    return lax.shift_right_logical(value * 16843009, 24)


def tile_tables(key):
    folded = jax.random.fold_in(key, 11)
    keys = jax.random.split(folded, 6)
    blocks = jnp.arange(ROWBLOCKS, dtype=jnp.int32)
    base_draw = jax.random.randint(keys[0], (ROWBLOCKS,), 0, TPR, dtype=jnp.int32)
    heaviness = jax.random.randint(keys[1], (N_DOM,), 2, 7, dtype=jnp.int32)
    counts = jnp.minimum(TPR, 1 + base_draw * heaviness[blocks // PBLK] // 4)
    picked = jax.random.randint(keys[2], (N_DOM * N_GRP,), 0, DBLK, dtype=jnp.int32)
    filled = blocks % DBLK == picked[blocks // DBLK]
    counts = jnp.where(filled, TPR, counts).astype(jnp.int32)
    shape = (ROWBLOCKS, TPR, TILE * TILE // 8)
    packed = jax.random.randint(keys[3], shape, 0, 256, dtype=jnp.int32)
    for layer in range(4):
        packed = packed & jax.random.randint(jax.random.fold_in(keys[4], layer), shape, 0, 256, dtype=jnp.int32)
    packed = packed.at[0, 0, 0].set(255).at[0, 0, 1].set(0)
    ones = count_bits(packed).reshape(ROWBLOCKS, TPR, TILE, TILE // 8).sum(-1)
    live_mask = (jnp.arange(TPR, dtype=jnp.int32)[None, :] < counts[:, None]).astype(jnp.int32)
    row_ones = (ones * live_mask[:, :, None]).sum(1).reshape(-1)
    degree = row_ones + jax.random.randint(keys[5], (NODES,), 1, 9, dtype=jnp.int32)
    degree = degree.at[0].set(TPR * TILE + 8)
    return (counts, packed, degree.astype(jnp.int32))


def draw_tile_count(key, part):
    return tile_tables(key)[0]


def draw_adjacency(key, part):
    return tile_tables(key)[1]


def draw_degree(key, part):
    return tile_tables(key)[2]


def plant(result, stream_key, least, largest):
    extent = result.shape
    index_at = [jax.random.randint(jax.random.fold_in(stream_key, axis), (), 0, extent[axis]) for axis in range(len(extent))]
    result = result.at[tuple(index_at)].set(least)
    longest = extent.index(max(extent))
    index_at[longest] = (index_at[longest] + 1) % extent[longest]
    return result.at[tuple(index_at)].set(largest)


def block_scale(key, shape, cuts, smallest, high):
    def one(axis_at, shards_of):
        heights = jax.random.uniform(jax.random.fold_in(jax.random.fold_in(key, 6), axis_at), (shards_of,), jnp.float32, smallest / len(cuts), high / len(cuts))
        return jnp.repeat(jnp.exp(heights), shape[axis_at] // shards_of).reshape((-1,) + (1,) * (len(shape) - axis_at - 1))

    factor_of = one(*cuts[0])
    for cut in cuts[1:]:
        factor_of = factor_of * one(*cut)
    return factor_of


def scatter_about(own_key, shape, spread, limit, cuts=(), kind=jnp.bfloat16):
    factor_of = block_scale(own_key, shape, cuts, -0.22, 0.18) if cuts else 1.0
    drawn = jax.random.normal(own_key, shape, jnp.float32) * spread * factor_of
    return jnp.minimum(jnp.maximum(drawn, -limit), limit).astype(kind)


def setup_inputs(seed: int = 0) -> dict:
    key_list = jax.random.split(jax.random.key(seed), 11)
    return {
        "x_current": scatter_about(key_list[0], (NODES, F), 1.0, 6.0, ((0, 32),)),
        "x_cached": scatter_about(key_list[1], (NODES, F), 1.0, 6.0, ((0, 32),)),
        "w_self": scatter_about(key_list[2], (F, H), F ** -0.5, 0.5),
        "w_neigh": scatter_about(key_list[3], (F, H), (F // 4) ** -0.5, 1.0),
        "bias": scatter_about(key_list[4], (H,), 0.5, 3.0, (), jnp.float32),
        "tile_columns": plant(jax.random.randint(key_list[5], (ROWBLOCKS, TPR), 0, PBLK + N_DOM * N_GRP * BB), jax.random.fold_in(key_list[5], 1), 0, (PBLK + N_DOM * N_GRP * BB) - 1).astype(jnp.int32),
        "tile_count": draw_tile_count(jax.random.fold_in(key_list[10], 71), 0),
        "adjacency": draw_adjacency(jax.random.fold_in(key_list[10], 71), 0),
        "degree": draw_degree(jax.random.fold_in(key_list[10], 71), 0),
        "boundary_blocks": plant(jax.random.randint(key_list[9], (N_DOM * N_GRP, BB), 0, DBLK), jax.random.fold_in(key_list[9], 1), 0, DBLK - 1).astype(jnp.int32),
    }


def block_sums(block_table, columns, counts, packed, rowblock_ids):
    group_size = columns.shape[0]
    shifts = jnp.arange(8, dtype=jnp.int32)
    bit_values = (packed.reshape(group_size, TPR, TILE, TILE // 8, 1) >> shifts) & 1
    live_mask = (jnp.arange(TPR, dtype=jnp.int32)[None, :] < counts[:, None]).astype(jnp.int32)
    adjacent = (bit_values.reshape(group_size, TPR, TILE, TILE) * live_mask[:, :, None, None]).astype(jnp.float32)
    partition = rowblock_ids // PBLK
    index_rows = jnp.where(columns < PBLK, partition[:, None] * PBLK + columns, ROWBLOCKS + columns - PBLK).astype(jnp.int32)
    gathered = block_table[index_rows].astype(jnp.float32)
    return jnp.einsum("stij,stjf->sif", adjacent, gathered)


def reference(x_current, x_cached, w_self, w_neigh, bias, tile_columns, tile_count, adjacency, degree, boundary_blocks):
    devices = N_DOM * N_GRP
    cached_blocks = x_cached.reshape(ROWBLOCKS, TILE, F)
    device_base = jnp.arange(devices, dtype=jnp.int32) * DBLK
    halo_blocks = cached_blocks[(device_base[:, None] + boundary_blocks).reshape(-1).astype(jnp.int32)]
    block_table = jnp.concatenate([x_current.reshape(ROWBLOCKS, TILE, F), halo_blocks], axis=0)
    group_size = 16 if ROWBLOCKS % 16 == 0 else 1
    turns = ROWBLOCKS // group_size
    rowblock_ids = jnp.arange(ROWBLOCKS, dtype=jnp.int32).reshape(turns, group_size)

    def one_group(pieces):
        return block_sums(block_table, pieces[0], pieces[1], pieces[2], pieces[3])

    totals = lax.map(one_group, (tile_columns.reshape(turns, group_size, TPR), tile_count.reshape(turns, group_size), adjacency.reshape(turns, group_size, TPR, -1), rowblock_ids))
    totals = totals.reshape(NODES, F)
    average = (totals / degree.astype(jnp.float32)[:, None]).astype(jnp.bfloat16)
    summed = jnp.dot(x_current, w_self, preferred_element_type=jnp.float32) + jnp.dot(average, w_neigh, preferred_element_type=jnp.float32) + bias
    return jnp.maximum(summed, 0.0).astype(jnp.bfloat16)
```

```python
import functools

import jax
import jax.numpy as jnp
from jax import lax
from jax.experimental import pallas as pl
from jax.experimental.pallas import tpu as pltpu
from jax.sharding import PartitionSpec as P

CHUNK = 8


def _expand_matrix(tile, dtype):
    words = tile // 8
    lanes = tile
    rows = lax.broadcasted_iota(jnp.int32, (lanes, 8 * tile), 0)
    cols = lax.broadcasted_iota(jnp.int32, (lanes, 8 * tile), 1)
    s = cols // tile
    j = cols % tile
    hit = rows == words * s + j // 8
    scale = lax.shift_left(jnp.int32(1), 7 - j % 8).astype(jnp.float32)
    return jnp.where(hit, scale, 0.0).astype(dtype)


def _perm_matrix(tile, dtype):
    kk = tile // 8
    rows = lax.broadcasted_iota(jnp.int32, (tile, tile), 0)
    cols = lax.broadcasted_iota(jnp.int32, (tile, tile), 1)
    return (rows == 8 * (cols % kk) + cols // kk).astype(dtype)


def _layer_kernel(cols_ref, counts_ref, adj_ref, table_ref, xc_ref, deg_ref, w_ref, b_ref,
                  mexp_ref, perm_ref, out_ref, *, per_tile, tile, n_table):
    r = pl.program_id(0)
    count = counts_ref[r]
    n_chunks = (count + CHUNK - 1) // CHUNK
    kk = tile // 8

    def chunk_body(c, acc):
        start = pl.multiple_of(c * (CHUNK * kk), CHUNK * kk)
        words = adj_ref[0, pl.ds(start, CHUNK * kk), :]
        spread = jnp.dot(words.astype(jnp.bfloat16), mexp_ref[...],
                         preferred_element_type=jnp.float32)
        bits = (spread.astype(jnp.int32) & 128).astype(jnp.bfloat16)
        rows = []
        for s in range(8):
            rows.append(jnp.concatenate(
                [bits[tl * kk:(tl + 1) * kk, s * tile:(s + 1) * tile] for tl in range(CHUNK)],
                axis=1))
        a_cat = jnp.concatenate(rows, axis=0)
        xs = []
        for tl in range(CHUNK):
            t = c * CHUNK + tl
            col = jnp.minimum(cols_ref[r * per_tile + t], n_table - 1)
            xt = table_ref[col]
            xs.append(jnp.where(t < count, xt, jnp.zeros_like(xt)))
        x_cat = jnp.concatenate(xs, axis=0)
        return acc + jnp.dot(a_cat, x_cat, preferred_element_type=jnp.float32)

    acc = lax.fori_loop(0, n_chunks, chunk_body, jnp.zeros((tile, tile), jnp.float32))
    totals = acc * (1.0 / 128.0)
    avg_perm = (totals / deg_ref[...]).astype(jnp.bfloat16)
    avg = jnp.dot(perm_ref[...], avg_perm, preferred_element_type=jnp.float32).astype(jnp.bfloat16)
    lhs = jnp.concatenate([xc_ref[...], avg], axis=1)
    summed = jnp.dot(lhs, w_ref[...], preferred_element_type=jnp.float32) + b_ref[...]
    out_ref[...] = jnp.maximum(summed, 0.0).astype(out_ref.dtype)


def on_device(
    x_current,
    x_cached,
    w_self,
    w_neigh,
    bias,
    tile_columns,
    tile_count,
    adjacency,
    degree,
    boundary_blocks,
):
    node_rows, width = x_current.shape
    row_blocks, per_tile = tile_columns.shape
    tile_rows = node_rows // row_blocks
    hidden = w_self.shape[1]
    kk = tile_rows // 8
    assert per_tile % CHUNK == 0
    chosen = x_cached.reshape(row_blocks, tile_rows, width)[boundary_blocks[0]]
    received = lax.all_gather(x_current, "grp", axis=0, tiled=True)
    part_blocks = received.reshape(-1, tile_rows, width)
    partial_value = lax.all_gather(chosen[None, None], "grp", axis=1, tiled=True)
    halo_blocks = lax.all_gather(partial_value, "dom", axis=0, tiled=True)
    block_table = jnp.concatenate([part_blocks, halo_blocks.reshape(-1, tile_rows, width)], axis=0)
    n_table = block_table.shape[0]

    adj = adjacency.reshape(row_blocks, per_tile * kk, tile_rows)
    deg = (degree.astype(jnp.float32).reshape(row_blocks, kk, 8)
           .transpose(0, 2, 1).reshape(node_rows, 1))
    w_cat = jnp.concatenate([w_self, w_neigh], axis=0)
    b2 = bias.reshape(1, hidden)
    mexp = _expand_matrix(tile_rows, jnp.bfloat16)
    perm = _perm_matrix(tile_rows, jnp.bfloat16)
    cols_flat = tile_columns.reshape(-1)

    kernel = functools.partial(_layer_kernel, per_tile=per_tile, tile=tile_rows, n_table=n_table)
    grid_spec = pltpu.PrefetchScalarGridSpec(
        num_scalar_prefetch=2,
        grid=(row_blocks,),
        in_specs=[
            pl.BlockSpec((1, per_tile * kk, tile_rows), lambda r, *_: (r, 0, 0)),
            pl.BlockSpec((n_table, tile_rows, width), lambda r, *_: (0, 0, 0)),
            pl.BlockSpec((tile_rows, width), lambda r, *_: (r, 0)),
            pl.BlockSpec((tile_rows, 1), lambda r, *_: (r, 0)),
            pl.BlockSpec((2 * width, hidden), lambda r, *_: (0, 0)),
            pl.BlockSpec((1, hidden), lambda r, *_: (0, 0)),
            pl.BlockSpec((tile_rows, 8 * tile_rows), lambda r, *_: (0, 0)),
            pl.BlockSpec((tile_rows, tile_rows), lambda r, *_: (0, 0)),
        ],
        out_specs=pl.BlockSpec((tile_rows, hidden), lambda r, *_: (r, 0)),
    )
    return pl.pallas_call(
        kernel,
        grid_spec=grid_spec,
        out_shape=jax.ShapeDtypeStruct((node_rows, hidden), jnp.bfloat16),
        compiler_params=pltpu.CompilerParams(
            dimension_semantics=("arbitrary",), vmem_limit_bytes=48 * 1024 * 1024),
    )(cols_flat, tile_count, adj, block_table, x_current, deg, w_cat, b2, mexp, perm)


def solution(mesh):
    in_specs = (
        P(("dom", "grp"), None),
        P(("dom", "grp"), None),
        P(),
        P(),
        P(),
        P(("dom", "grp"), None),
        P(("dom", "grp")),
        P(("dom", "grp"), None, None),
        P(("dom", "grp")),
        P(("dom", "grp"), None),
    )
    out_specs = P(("dom", "grp"), None)
    return jax.shard_map(
        on_device, mesh=mesh, in_specs=in_specs, out_specs=out_specs, check_vma=False
    )
```

```python
import functools

import jax
import jax.numpy as jnp
from jax import lax
from jax.experimental import pallas as pl
from jax.experimental.pallas import tpu as pltpu
from jax.sharding import PartitionSpec as P

CHUNK = 8


def _expand_matrix(tile, dtype):
    words = tile // 8
    lanes = tile
    rows = lax.broadcasted_iota(jnp.int32, (lanes, 8 * tile), 0)
    cols = lax.broadcasted_iota(jnp.int32, (lanes, 8 * tile), 1)
    s = cols // tile
    j = cols % tile
    hit = rows == words * s + j // 8
    scale = lax.shift_left(jnp.int32(1), 7 - j % 8).astype(jnp.float32)
    return jnp.where(hit, scale, 0.0).astype(dtype)


def _perm_matrix(tile, dtype):
    kk = tile // 8
    rows = lax.broadcasted_iota(jnp.int32, (tile, tile), 0)
    cols = lax.broadcasted_iota(jnp.int32, (tile, tile), 1)
    return (rows == 8 * (cols % kk) + cols // kk).astype(dtype)


def _layer_kernel(cols_ref, counts_ref, grp_ref, adj_ref, xc_ref, deg_ref, w_ref, b_ref,
                  mexp_ref, perm_ref, *rest, per_tile, tile, n_table, n_grp, dev_blocks):
    pieces = rest[:n_grp + 1]
    out_ref, table_ref, sems = rest[n_grp + 1:]
    r = pl.program_id(0)
    count = counts_ref[r]
    g = grp_ref[0]
    part = n_grp * dev_blocks

    @pl.when(r == 0)
    def _():
        copies = []
        for d in range(n_grp):
            copies.append(pltpu.make_async_copy(
                pieces[d], table_ref.at[pl.ds(d * dev_blocks, dev_blocks)], sems.at[d]))
        n_halo = n_table - part
        copies.append(pltpu.make_async_copy(
            pieces[n_grp], table_ref.at[pl.ds(part, n_halo)], sems.at[n_grp]))
        for cp in copies:
            cp.start()
        for cp in copies:
            cp.wait()

    n_chunks = (count + CHUNK - 1) // CHUNK
    kk = tile // 8

    def chunk_body(c, acc):
        start = pl.multiple_of(c * (CHUNK * kk), CHUNK * kk)
        words = adj_ref[0, pl.ds(start, CHUNK * kk), :]
        spread = jnp.dot(words.astype(jnp.bfloat16), mexp_ref[...],
                         preferred_element_type=jnp.float32)
        bits = (spread.astype(jnp.int32) & 128).astype(jnp.bfloat16)
        rows = []
        for s in range(8):
            rows.append(jnp.concatenate(
                [bits[tl * kk:(tl + 1) * kk, s * tile:(s + 1) * tile] for tl in range(CHUNK)],
                axis=1))
        a_cat = jnp.concatenate(rows, axis=0)
        xs = []
        for tl in range(CHUNK):
            t = c * CHUNK + tl
            col = cols_ref[r * per_tile + t]
            rel = ((g - col // dev_blocks + n_grp) % n_grp) * dev_blocks + col % dev_blocks
            col = jnp.clip(jnp.where(col < part, rel, col), 0, n_table - 1)
            xt = table_ref[col]
            xs.append(jnp.where(t < count, xt, jnp.zeros_like(xt)))
        x_cat = jnp.concatenate(xs, axis=0)
        return acc + jnp.dot(a_cat, x_cat, preferred_element_type=jnp.float32)

    acc = lax.fori_loop(0, n_chunks, chunk_body, jnp.zeros((tile, tile), jnp.float32))
    totals = acc * (1.0 / 128.0)
    avg_perm = (totals / deg_ref[...]).astype(jnp.bfloat16)
    avg = jnp.dot(perm_ref[...], avg_perm, preferred_element_type=jnp.float32).astype(jnp.bfloat16)
    lhs = jnp.concatenate([xc_ref[...], avg], axis=1)
    summed = jnp.dot(lhs, w_ref[...], preferred_element_type=jnp.float32) + b_ref[...]
    out_ref[...] = jnp.maximum(summed, 0.0).astype(out_ref.dtype)


def on_device(
    x_current,
    x_cached,
    w_self,
    w_neigh,
    bias,
    tile_columns,
    tile_count,
    adjacency,
    degree,
    boundary_blocks,
):
    node_rows, width = x_current.shape
    row_blocks, per_tile = tile_columns.shape
    tile_rows = node_rows // row_blocks
    hidden = w_self.shape[1]
    kk = tile_rows // 8
    assert per_tile % CHUNK == 0
    n_grp = lax.psum(1, "grp")
    chosen = x_cached.reshape(row_blocks, tile_rows, width)[boundary_blocks[0]]
    halo_blocks = lax.all_gather(chosen, ("dom", "grp"), axis=0, tiled=True)
    own_blocks = x_current.reshape(row_blocks, tile_rows, width)
    pieces = [own_blocks]
    for d in range(1, n_grp):
        pieces.append(lax.ppermute(own_blocks, "grp", [(i, (i + d) % n_grp) for i in range(n_grp)]))
    pieces.append(halo_blocks)
    n_table = n_grp * row_blocks + halo_blocks.shape[0]
    grp_idx = jnp.full((1,), lax.axis_index("grp"), jnp.int32)

    adj = adjacency.reshape(row_blocks, per_tile * kk, tile_rows)
    deg = (degree.astype(jnp.float32).reshape(row_blocks, kk, 8)
           .transpose(0, 2, 1).reshape(node_rows, 1))
    w_cat = jnp.concatenate([w_self, w_neigh], axis=0)
    b2 = bias.reshape(1, hidden)
    mexp = _expand_matrix(tile_rows, jnp.bfloat16)
    perm = _perm_matrix(tile_rows, jnp.bfloat16)
    cols_flat = tile_columns.reshape(-1)

    kernel = functools.partial(_layer_kernel, per_tile=per_tile, tile=tile_rows, n_table=n_table,
                               n_grp=n_grp, dev_blocks=row_blocks)
    grid_spec = pltpu.PrefetchScalarGridSpec(
        num_scalar_prefetch=3,
        grid=(row_blocks,),
        in_specs=[
            pl.BlockSpec((1, per_tile * kk, tile_rows), lambda r, *_: (r, 0, 0)),
            pl.BlockSpec((tile_rows, width), lambda r, *_: (r, 0)),
            pl.BlockSpec((tile_rows, 1), lambda r, *_: (r, 0)),
            pl.BlockSpec((2 * width, hidden), lambda r, *_: (0, 0)),
            pl.BlockSpec((1, hidden), lambda r, *_: (0, 0)),
            pl.BlockSpec((tile_rows, 8 * tile_rows), lambda r, *_: (0, 0)),
            pl.BlockSpec((tile_rows, tile_rows), lambda r, *_: (0, 0)),
        ] + [pl.BlockSpec(memory_space=pl.ANY)] * (n_grp + 1),
        out_specs=pl.BlockSpec((tile_rows, hidden), lambda r, *_: (r, 0)),
        scratch_shapes=[pltpu.VMEM((n_table, tile_rows, width), jnp.bfloat16),
                        pltpu.SemaphoreType.DMA((n_grp + 1,))],
    )
    return pl.pallas_call(
        kernel,
        grid_spec=grid_spec,
        out_shape=jax.ShapeDtypeStruct((node_rows, hidden), jnp.bfloat16),
        compiler_params=pltpu.CompilerParams(
            dimension_semantics=("arbitrary",), vmem_limit_bytes=48 * 1024 * 1024),
    )(cols_flat, tile_count, grp_idx, adj, x_current, deg, w_cat, b2, mexp, perm, *pieces)


def solution(mesh):
    in_specs = (
        P(("dom", "grp"), None),
        P(("dom", "grp"), None),
        P(),
        P(),
        P(),
        P(("dom", "grp"), None),
        P(("dom", "grp")),
        P(("dom", "grp"), None, None),
        P(("dom", "grp")),
        P(("dom", "grp"), None),
    )
    out_specs = P(("dom", "grp"), None)
    return jax.shard_map(
        on_device, mesh=mesh, in_specs=in_specs, out_specs=out_specs, check_vma=False
    )
```

```python
import functools

import jax
import jax.numpy as jnp
from jax import lax
from jax.experimental import pallas as pl
from jax.experimental.pallas import tpu as pltpu
from jax.sharding import PartitionSpec as P

CHUNK = 8


def _expand_matrix(tile, dtype):
    words = tile // 8
    lanes = tile
    rows = lax.broadcasted_iota(jnp.int32, (lanes, 8 * tile), 0)
    cols = lax.broadcasted_iota(jnp.int32, (lanes, 8 * tile), 1)
    s = cols // tile
    j = cols % tile
    hit = rows == words * s + j // 8
    scale = lax.shift_left(jnp.int32(1), 7 - j % 8).astype(jnp.float32)
    return jnp.where(hit, scale, 0.0).astype(dtype)


def _perm_matrix(tile, dtype):
    kk = tile // 8
    rows = lax.broadcasted_iota(jnp.int32, (tile, tile), 0)
    cols = lax.broadcasted_iota(jnp.int32, (tile, tile), 1)
    return (rows == 8 * (cols % kk) + cols // kk).astype(dtype)


def _layer_kernel(cols_ref, counts_ref, grp_ref, adj_ref, xc_ref, deg_ref, w_ref, b_ref,
                  mexp_ref, perm_ref, *rest, per_tile, tile, n_table, n_grp, dev_blocks):
    pieces = rest[:n_grp + 1]
    out_ref, table_ref, sems = rest[n_grp + 1:]
    r = pl.program_id(0)
    count = counts_ref[r]
    g = grp_ref[0]
    part = n_grp * dev_blocks

    @pl.when(r == 0)
    def _():
        copies = []
        for d in range(n_grp):
            copies.append(pltpu.make_async_copy(
                pieces[d], table_ref.at[pl.ds(d * dev_blocks, dev_blocks)], sems.at[d]))
        n_halo = n_table - part
        copies.append(pltpu.make_async_copy(
            pieces[n_grp], table_ref.at[pl.ds(part, n_halo)], sems.at[n_grp]))
        for cp in copies:
            cp.start()
        for cp in copies:
            cp.wait()

    n_chunks = (count + CHUNK - 1) // CHUNK
    kk = tile // 8

    def chunk_body(c, acc):
        start = pl.multiple_of(c * (CHUNK * kk), CHUNK * kk)
        words = adj_ref[0, pl.ds(start, CHUNK * kk), :]
        spread = jnp.dot(words.astype(jnp.bfloat16), mexp_ref[...],
                         preferred_element_type=jnp.float32)
        bits = (spread.astype(jnp.int32) & 128).astype(jnp.bfloat16)
        rows = []
        for s in range(8):
            rows.append(jnp.concatenate(
                [bits[tl * kk:(tl + 1) * kk, s * tile:(s + 1) * tile] for tl in range(CHUNK)],
                axis=1))
        a_cat = jnp.concatenate(rows, axis=0)
        xs = []
        for tl in range(CHUNK):
            t = c * CHUNK + tl
            col = cols_ref[r, t]
            if n_grp == 4:
                slot = jnp.bitwise_xor(col // dev_blocks, g)
            else:
                slot = (g - col // dev_blocks + n_grp) % n_grp
            rel = slot * dev_blocks + col % dev_blocks
            col = jnp.clip(jnp.where(col < part, rel, col), 0, n_table - 1)
            xt = table_ref[col]
            xs.append(jnp.where(t < count, xt, jnp.zeros_like(xt)))
        x_cat = jnp.concatenate(xs, axis=0)
        return acc + jnp.dot(a_cat, x_cat, preferred_element_type=jnp.float32)

    acc = lax.fori_loop(0, n_chunks, chunk_body, jnp.zeros((tile, tile), jnp.float32))
    totals = acc * (1.0 / 128.0)
    deg_row = deg_ref[pl.ds(r, 1), :].astype(jnp.float32)
    pick = perm_ref[...].T > 0
    deg_perm = jnp.sum(jnp.where(pick, deg_row, 0.0), axis=1, keepdims=True)
    avg_perm = (totals / deg_perm).astype(jnp.bfloat16)
    avg = jnp.dot(perm_ref[...], avg_perm, preferred_element_type=jnp.float32).astype(jnp.bfloat16)
    lhs = jnp.concatenate([xc_ref[...], avg], axis=1)
    summed = jnp.dot(lhs, w_ref[...], preferred_element_type=jnp.float32) + b_ref[...]
    out_ref[...] = jnp.maximum(summed, 0.0).astype(out_ref.dtype)


def on_device(
    x_current,
    x_cached,
    w_self,
    w_neigh,
    bias,
    tile_columns,
    tile_count,
    adjacency,
    degree,
    boundary_blocks,
):
    node_rows, width = x_current.shape
    row_blocks, per_tile = tile_columns.shape
    tile_rows = node_rows // row_blocks
    hidden = w_self.shape[1]
    kk = tile_rows // 8
    assert per_tile % CHUNK == 0
    n_grp = lax.psum(1, "grp")
    chosen = x_cached.reshape(row_blocks, tile_rows, width)[boundary_blocks[0]]
    halo_blocks = lax.all_gather(chosen, ("dom", "grp"), axis=0, tiled=True)
    own_blocks = x_current.reshape(row_blocks, tile_rows, width)
    pieces = [own_blocks]
    if n_grp == 4:
        near = lax.ppermute(own_blocks, "grp", [(i, i ^ 1) for i in range(4)])
        far = lax.ppermute(own_blocks, "grp", [(i, i ^ 2) for i in range(4)])
        far_near = lax.ppermute(far, "grp", [(i, i ^ 1) for i in range(4)])
        pieces += [near, far, far_near]
    else:
        for d in range(1, n_grp):
            pieces.append(lax.ppermute(own_blocks, "grp", [(i, (i + d) % n_grp) for i in range(n_grp)]))
    pieces.append(halo_blocks)
    n_table = n_grp * row_blocks + halo_blocks.shape[0]
    grp_idx = jnp.full((1,), lax.axis_index("grp"), jnp.int32)

    adj = adjacency.reshape(row_blocks, per_tile * kk, tile_rows)
    deg = degree.reshape(row_blocks, tile_rows)
    w_cat = jnp.concatenate([w_self, w_neigh], axis=0)
    b2 = bias.reshape(1, hidden)
    mexp = _expand_matrix(tile_rows, jnp.bfloat16)
    perm = _perm_matrix(tile_rows, jnp.bfloat16)

    kernel = functools.partial(_layer_kernel, per_tile=per_tile, tile=tile_rows, n_table=n_table,
                               n_grp=n_grp, dev_blocks=row_blocks)
    grid_spec = pltpu.PrefetchScalarGridSpec(
        num_scalar_prefetch=3,
        grid=(row_blocks,),
        in_specs=[
            pl.BlockSpec((1, per_tile * kk, tile_rows), lambda r, *_: (r, 0, 0)),
            pl.BlockSpec((tile_rows, width), lambda r, *_: (r, 0)),
            pl.BlockSpec((row_blocks, tile_rows), lambda r, *_: (0, 0)),
            pl.BlockSpec((2 * width, hidden), lambda r, *_: (0, 0)),
            pl.BlockSpec((1, hidden), lambda r, *_: (0, 0)),
            pl.BlockSpec((tile_rows, 8 * tile_rows), lambda r, *_: (0, 0)),
            pl.BlockSpec((tile_rows, tile_rows), lambda r, *_: (0, 0)),
        ] + [pl.BlockSpec(memory_space=pl.ANY)] * (n_grp + 1),
        out_specs=pl.BlockSpec((tile_rows, hidden), lambda r, *_: (r, 0)),
        scratch_shapes=[pltpu.VMEM((n_table, tile_rows, width), jnp.bfloat16),
                        pltpu.SemaphoreType.DMA((n_grp + 1,))],
    )
    return pl.pallas_call(
        kernel,
        grid_spec=grid_spec,
        out_shape=jax.ShapeDtypeStruct((node_rows, hidden), jnp.bfloat16),
        compiler_params=pltpu.CompilerParams(
            dimension_semantics=("arbitrary",), vmem_limit_bytes=48 * 1024 * 1024),
    )(tile_columns, tile_count, grp_idx, adj, x_current, deg, w_cat, b2, mexp, perm, *pieces)


def solution(mesh):
    in_specs = (
        P(("dom", "grp"), None),
        P(("dom", "grp"), None),
        P(),
        P(),
        P(),
        P(("dom", "grp"), None),
        P(("dom", "grp")),
        P(("dom", "grp"), None, None),
        P(("dom", "grp")),
        P(("dom", "grp"), None),
    )
    out_specs = P(("dom", "grp"), None)
    return jax.shard_map(
        on_device, mesh=mesh, in_specs=in_specs, out_specs=out_specs, check_vma=False
    )
```

```python
import functools

import jax
import jax.numpy as jnp
from jax import lax
from jax.experimental import pallas as pl
from jax.experimental.pallas import tpu as pltpu
from jax.sharding import PartitionSpec as P

CHUNK = 8


def _expand_matrix(tile, dtype):
    words = tile // 8
    lanes = tile
    rows = lax.broadcasted_iota(jnp.int32, (lanes, 8 * tile), 0)
    cols = lax.broadcasted_iota(jnp.int32, (lanes, 8 * tile), 1)
    s = cols // tile
    j = cols % tile
    hit = rows == words * s + j // 8
    scale = lax.shift_left(jnp.int32(1), 7 - j % 8).astype(jnp.float32)
    return jnp.where(hit, scale, 0.0).astype(dtype)


def _perm_matrix(tile, dtype):
    kk = tile // 8
    rows = lax.broadcasted_iota(jnp.int32, (tile, tile), 0)
    cols = lax.broadcasted_iota(jnp.int32, (tile, tile), 1)
    return (rows == 8 * (cols % kk) + cols // kk).astype(dtype)


def _layer_kernel(cols_ref, counts_ref, grp_ref, adj_ref, xc_ref, deg_ref, w_ref, b_ref,
                  mexp_ref, perm_ref, *rest, per_tile, tile, n_table, n_grp, dev_blocks,
                  levels, per_dev):
    pieces = rest[:n_grp + 1]
    out_ref, table_ref, sems = rest[n_grp + 1:]
    r = pl.program_id(0)
    count = counts_ref[r]
    g = grp_ref[0]
    me = grp_ref[1]
    part = n_grp * dev_blocks

    @pl.when(r == 0)
    def _():
        copies = []
        for d in range(n_grp):
            copies.append(pltpu.make_async_copy(
                pieces[d], table_ref.at[pl.ds(d * dev_blocks, dev_blocks)], sems.at[d]))
        n_halo = n_table - part
        copies.append(pltpu.make_async_copy(
            pieces[n_grp], table_ref.at[pl.ds(part, n_halo)], sems.at[n_grp]))
        for cp in copies:
            cp.start()
        for cp in copies:
            cp.wait()

    n_chunks = (count + CHUNK - 1) // CHUNK
    kk = tile // 8

    def chunk_body(c, acc):
        start = pl.multiple_of(c * (CHUNK * kk), CHUNK * kk)
        words = adj_ref[0, pl.ds(start, CHUNK * kk), :]
        spread = jnp.dot(words.astype(jnp.bfloat16), mexp_ref[...],
                         preferred_element_type=jnp.float32)
        bits = (spread.astype(jnp.int32) & 128).astype(jnp.bfloat16)
        rows = []
        for s in range(8):
            rows.append(jnp.concatenate(
                [bits[tl * kk:(tl + 1) * kk, s * tile:(s + 1) * tile] for tl in range(CHUNK)],
                axis=1))
        a_cat = jnp.concatenate(rows, axis=0)
        xs = []
        for tl in range(CHUNK):
            t = c * CHUNK + tl
            col = cols_ref[r, t]
            if n_grp == 4:
                slot = jnp.bitwise_xor(col // dev_blocks, g)
            else:
                slot = (g - col // dev_blocks + n_grp) % n_grp
            rel = slot * dev_blocks + col % dev_blocks
            h = jnp.maximum(col - part, 0)
            x = jnp.bitwise_xor(h // per_dev, me)
            pos = jnp.int32(0)
            for bit in range(levels):
                pos = pos + ((x >> bit) & 1) * (1 << (levels - 1 - bit))
            hrel = part + pos * per_dev + h % per_dev
            col = jnp.clip(jnp.where(col < part, rel, hrel), 0, n_table - 1)
            xt = table_ref[col]
            xs.append(jnp.where(t < count, xt, jnp.zeros_like(xt)))
        x_cat = jnp.concatenate(xs, axis=0)
        return acc + jnp.dot(a_cat, x_cat, preferred_element_type=jnp.float32)

    acc = lax.fori_loop(0, n_chunks, chunk_body, jnp.zeros((tile, tile), jnp.float32))
    totals = acc * (1.0 / 128.0)
    deg_row = deg_ref[pl.ds(r, 1), :].astype(jnp.float32)
    pick = perm_ref[...].T > 0
    deg_perm = jnp.sum(jnp.where(pick, deg_row, 0.0), axis=1, keepdims=True)
    avg_perm = (totals / deg_perm).astype(jnp.bfloat16)
    avg = jnp.dot(perm_ref[...], avg_perm, preferred_element_type=jnp.float32).astype(jnp.bfloat16)
    lhs = jnp.concatenate([xc_ref[...], avg], axis=1)
    summed = jnp.dot(lhs, w_ref[...], preferred_element_type=jnp.float32) + b_ref[...]
    out_ref[...] = jnp.maximum(summed, 0.0).astype(out_ref.dtype)


def on_device(
    x_current,
    x_cached,
    w_self,
    w_neigh,
    bias,
    tile_columns,
    tile_count,
    adjacency,
    degree,
    boundary_blocks,
):
    node_rows, width = x_current.shape
    row_blocks, per_tile = tile_columns.shape
    tile_rows = node_rows // row_blocks
    hidden = w_self.shape[1]
    kk = tile_rows // 8
    assert per_tile % CHUNK == 0
    n_grp = lax.psum(1, "grp")
    chosen = x_cached.reshape(row_blocks, tile_rows, width)[boundary_blocks[0]]
    n_dom = lax.psum(1, "dom")
    n_dev = n_dom * n_grp
    levels = n_dev.bit_length() - 1
    assert 1 << levels == n_dev
    me = lax.axis_index("dom") * n_grp + lax.axis_index("grp")
    halo_blocks = chosen
    for lv in range(levels):
        mask = n_dev >> (lv + 1)
        theirs = lax.ppermute(halo_blocks, ("dom", "grp"), [(i, i ^ mask) for i in range(n_dev)])
        halo_blocks = jnp.concatenate([halo_blocks, theirs], axis=0)
    own_blocks = x_current.reshape(row_blocks, tile_rows, width)
    pieces = [own_blocks]
    if n_grp == 4:
        near = lax.ppermute(own_blocks, "grp", [(i, i ^ 1) for i in range(4)])
        far = lax.ppermute(own_blocks, "grp", [(i, i ^ 2) for i in range(4)])
        far_near = lax.ppermute(far, "grp", [(i, i ^ 1) for i in range(4)])
        pieces += [near, far, far_near]
    else:
        for d in range(1, n_grp):
            pieces.append(lax.ppermute(own_blocks, "grp", [(i, (i + d) % n_grp) for i in range(n_grp)]))
    pieces.append(halo_blocks)
    n_table = n_grp * row_blocks + halo_blocks.shape[0]
    grp_idx = jnp.stack([lax.axis_index("grp"), me]).astype(jnp.int32)

    adj = adjacency.reshape(row_blocks, per_tile * kk, tile_rows)
    deg = degree.reshape(row_blocks, tile_rows)
    w_cat = jnp.concatenate([w_self, w_neigh], axis=0)
    b2 = bias.reshape(1, hidden)
    mexp = _expand_matrix(tile_rows, jnp.bfloat16)
    perm = _perm_matrix(tile_rows, jnp.bfloat16)

    kernel = functools.partial(_layer_kernel, per_tile=per_tile, tile=tile_rows, n_table=n_table,
                               n_grp=n_grp, dev_blocks=row_blocks, levels=levels,
                               per_dev=chosen.shape[0])
    grid_spec = pltpu.PrefetchScalarGridSpec(
        num_scalar_prefetch=3,
        grid=(row_blocks,),
        in_specs=[
            pl.BlockSpec((1, per_tile * kk, tile_rows), lambda r, *_: (r, 0, 0)),
            pl.BlockSpec((tile_rows, width), lambda r, *_: (r, 0)),
            pl.BlockSpec((row_blocks, tile_rows), lambda r, *_: (0, 0)),
            pl.BlockSpec((2 * width, hidden), lambda r, *_: (0, 0)),
            pl.BlockSpec((1, hidden), lambda r, *_: (0, 0)),
            pl.BlockSpec((tile_rows, 8 * tile_rows), lambda r, *_: (0, 0)),
            pl.BlockSpec((tile_rows, tile_rows), lambda r, *_: (0, 0)),
        ] + [pl.BlockSpec(memory_space=pl.ANY)] * (n_grp + 1),
        out_specs=pl.BlockSpec((tile_rows, hidden), lambda r, *_: (r, 0)),
        scratch_shapes=[pltpu.VMEM((n_table, tile_rows, width), jnp.bfloat16),
                        pltpu.SemaphoreType.DMA((n_grp + 1,))],
    )
    return pl.pallas_call(
        kernel,
        grid_spec=grid_spec,
        out_shape=jax.ShapeDtypeStruct((node_rows, hidden), jnp.bfloat16),
        compiler_params=pltpu.CompilerParams(
            dimension_semantics=("arbitrary",), vmem_limit_bytes=48 * 1024 * 1024),
    )(tile_columns, tile_count, grp_idx, adj, x_current, deg, w_cat, b2, mexp, perm, *pieces)


def solution(mesh):
    in_specs = (
        P(("dom", "grp"), None),
        P(("dom", "grp"), None),
        P(),
        P(),
        P(),
        P(("dom", "grp"), None),
        P(("dom", "grp")),
        P(("dom", "grp"), None, None),
        P(("dom", "grp")),
        P(("dom", "grp"), None),
    )
    out_specs = P(("dom", "grp"), None)
    return jax.shard_map(
        on_device, mesh=mesh, in_specs=in_specs, out_specs=out_specs, check_vma=False
    )
```

```python
import functools

import jax
import jax.numpy as jnp
from jax import lax
from jax.experimental import pallas as pl
from jax.experimental.pallas import tpu as pltpu
from jax.sharding import PartitionSpec as P

CHUNK = 8


def _expand_matrix(tile, dtype):
    words = tile // 8
    lanes = tile
    rows = lax.broadcasted_iota(jnp.int32, (lanes, 8 * tile), 0)
    cols = lax.broadcasted_iota(jnp.int32, (lanes, 8 * tile), 1)
    s = cols // tile
    j = cols % tile
    hit = rows == words * s + j // 8
    scale = lax.shift_left(jnp.int32(1), 7 - j % 8).astype(jnp.float32)
    return jnp.where(hit, scale, 0.0).astype(dtype)


def _perm_matrix(tile, dtype):
    kk = tile // 8
    rows = lax.broadcasted_iota(jnp.int32, (tile, tile), 0)
    cols = lax.broadcasted_iota(jnp.int32, (tile, tile), 1)
    return (rows == 8 * (cols % kk) + cols // kk).astype(dtype)


def _layer_kernel(cols_ref, counts_ref, grp_ref, adj_ref, xc_ref, deg_ref, w_ref, b_ref,
                  mexp_ref, perm_ref, *rest, per_tile, tile, n_table, n_grp, dev_blocks,
                  levels, per_dev):
    pieces = rest[:n_grp + 1]
    out_ref, table_ref, sems, words_ref, acc_ref = rest[n_grp + 1:]
    r = pl.program_id(0)
    count = counts_ref[r]
    g = grp_ref[0]
    me = grp_ref[1]
    part = n_grp * dev_blocks

    @pl.when(r == 0)
    def _():
        copies = []
        for d in range(n_grp):
            copies.append(pltpu.make_async_copy(
                pieces[d], table_ref.at[pl.ds(d * dev_blocks, dev_blocks)], sems.at[d]))
        n_halo = n_table - part
        copies.append(pltpu.make_async_copy(
            pieces[n_grp], table_ref.at[pl.ds(part, n_halo)], sems.at[n_grp]))
        for cp in copies:
            cp.start()
        for cp in copies:
            cp.wait()

    kk = tile // 8
    for k in range(kk):
        words_ref[pl.ds(k * per_tile, per_tile), :] = adj_ref[0, :, pl.ds(k * tile, tile)]
    acc_ref[...] = jnp.zeros_like(acc_ref)

    for c in range(per_tile // CHUNK):
        @pl.when(c * CHUNK < count)
        def _():
            words = jnp.concatenate(
                [words_ref[pl.ds(c * CHUNK + tl, kk, stride=per_tile), :] for tl in range(CHUNK)],
                axis=0)
            spread = jnp.dot(words.astype(jnp.bfloat16), mexp_ref[...],
                             preferred_element_type=jnp.float32)
            bits = (spread.astype(jnp.int32) & 128).astype(jnp.bfloat16)
            rows = []
            for s in range(8):
                rows.append(jnp.concatenate(
                    [bits[tl * kk:(tl + 1) * kk, s * tile:(s + 1) * tile] for tl in range(CHUNK)],
                    axis=1))
            a_cat = jnp.concatenate(rows, axis=0)
            xs = []
            for tl in range(CHUNK):
                t = c * CHUNK + tl
                col = cols_ref[r, t]
                if n_grp == 4:
                    slot = jnp.bitwise_xor(col // dev_blocks, g)
                else:
                    slot = (g - col // dev_blocks + n_grp) % n_grp
                rel = slot * dev_blocks + col % dev_blocks
                h = jnp.maximum(col - part, 0)
                x = jnp.bitwise_xor(h // per_dev, me)
                pos = jnp.int32(0)
                for bit in range(levels):
                    pos = pos + ((x >> bit) & 1) * (1 << (levels - 1 - bit))
                hrel = part + pos * per_dev + h % per_dev
                col = jnp.clip(jnp.where(col < part, rel, hrel), 0, n_table - 1)
                xt = table_ref[col]
                xs.append(jnp.where(t < count, xt, jnp.zeros_like(xt)))
            x_cat = jnp.concatenate(xs, axis=0)
            acc_ref[...] += jnp.dot(a_cat, x_cat, preferred_element_type=jnp.float32)

    acc = acc_ref[...]
    totals = acc * (1.0 / 128.0)
    deg_row = deg_ref[pl.ds(r, 1), :].astype(jnp.float32)
    pick = perm_ref[...].T > 0
    deg_perm = jnp.sum(jnp.where(pick, deg_row, 0.0), axis=1, keepdims=True)
    avg_perm = (totals / deg_perm).astype(jnp.bfloat16)
    avg = jnp.dot(perm_ref[...], avg_perm, preferred_element_type=jnp.float32).astype(jnp.bfloat16)
    lhs = jnp.concatenate([xc_ref[...], avg], axis=1)
    summed = jnp.dot(lhs, w_ref[...], preferred_element_type=jnp.float32) + b_ref[...]
    out_ref[...] = jnp.maximum(summed, 0.0).astype(out_ref.dtype)


def on_device(
    x_current,
    x_cached,
    w_self,
    w_neigh,
    bias,
    tile_columns,
    tile_count,
    adjacency,
    degree,
    boundary_blocks,
):
    node_rows, width = x_current.shape
    row_blocks, per_tile = tile_columns.shape
    tile_rows = node_rows // row_blocks
    hidden = w_self.shape[1]
    kk = tile_rows // 8
    assert per_tile % CHUNK == 0
    n_grp = lax.psum(1, "grp")
    chosen = x_cached.reshape(row_blocks, tile_rows, width)[boundary_blocks[0]]
    n_dom = lax.psum(1, "dom")
    n_dev = n_dom * n_grp
    levels = n_dev.bit_length() - 1
    assert 1 << levels == n_dev
    me = lax.axis_index("dom") * n_grp + lax.axis_index("grp")
    halo_blocks = chosen
    for lv in range(levels):
        mask = n_dev >> (lv + 1)
        theirs = lax.ppermute(halo_blocks, ("dom", "grp"), [(i, i ^ mask) for i in range(n_dev)])
        halo_blocks = jnp.concatenate([halo_blocks, theirs], axis=0)
    own_blocks = x_current.reshape(row_blocks, tile_rows, width)
    pieces = [own_blocks]
    if n_grp == 4:
        near = lax.ppermute(own_blocks, "grp", [(i, i ^ 1) for i in range(4)])
        far = lax.ppermute(own_blocks, "grp", [(i, i ^ 2) for i in range(4)])
        far_near = lax.ppermute(far, "grp", [(i, i ^ 1) for i in range(4)])
        pieces += [near, far, far_near]
    else:
        for d in range(1, n_grp):
            pieces.append(lax.ppermute(own_blocks, "grp", [(i, (i + d) % n_grp) for i in range(n_grp)]))
    pieces.append(halo_blocks)
    n_table = n_grp * row_blocks + halo_blocks.shape[0]
    grp_idx = jnp.stack([lax.axis_index("grp"), me]).astype(jnp.int32)

    deg = degree.reshape(row_blocks, tile_rows)
    w_cat = jnp.concatenate([w_self, w_neigh], axis=0)
    b2 = bias.reshape(1, hidden)
    mexp = _expand_matrix(tile_rows, jnp.bfloat16)
    perm = _perm_matrix(tile_rows, jnp.bfloat16)

    kernel = functools.partial(_layer_kernel, per_tile=per_tile, tile=tile_rows, n_table=n_table,
                               n_grp=n_grp, dev_blocks=row_blocks, levels=levels,
                               per_dev=chosen.shape[0])
    grid_spec = pltpu.PrefetchScalarGridSpec(
        num_scalar_prefetch=3,
        grid=(row_blocks,),
        in_specs=[
            pl.BlockSpec((1, per_tile, tile_rows * kk), lambda r, *_: (r, 0, 0)),
            pl.BlockSpec((tile_rows, width), lambda r, *_: (r, 0)),
            pl.BlockSpec((row_blocks, tile_rows), lambda r, *_: (0, 0)),
            pl.BlockSpec((2 * width, hidden), lambda r, *_: (0, 0)),
            pl.BlockSpec((1, hidden), lambda r, *_: (0, 0)),
            pl.BlockSpec((tile_rows, 8 * tile_rows), lambda r, *_: (0, 0)),
            pl.BlockSpec((tile_rows, tile_rows), lambda r, *_: (0, 0)),
        ] + [pl.BlockSpec(memory_space=pl.ANY)] * (n_grp + 1),
        out_specs=pl.BlockSpec((tile_rows, hidden), lambda r, *_: (r, 0)),
        scratch_shapes=[pltpu.VMEM((n_table, tile_rows, width), jnp.bfloat16),
                        pltpu.SemaphoreType.DMA((n_grp + 1,)),
                        pltpu.VMEM((per_tile * kk, tile_rows), jnp.int32),
                        pltpu.VMEM((tile_rows, width), jnp.float32)],
    )
    return pl.pallas_call(
        kernel,
        grid_spec=grid_spec,
        out_shape=jax.ShapeDtypeStruct((node_rows, hidden), jnp.bfloat16),
        compiler_params=pltpu.CompilerParams(
            dimension_semantics=("arbitrary",), vmem_limit_bytes=48 * 1024 * 1024),
    )(tile_columns, tile_count, grp_idx, adjacency, x_current, deg, w_cat, b2, mexp, perm, *pieces)


def solution(mesh):
    in_specs = (
        P(("dom", "grp"), None),
        P(("dom", "grp"), None),
        P(),
        P(),
        P(),
        P(("dom", "grp"), None),
        P(("dom", "grp")),
        P(("dom", "grp"), None, None),
        P(("dom", "grp")),
        P(("dom", "grp"), None),
    )
    out_specs = P(("dom", "grp"), None)
    return jax.shard_map(
        on_device, mesh=mesh, in_specs=in_specs, out_specs=out_specs, check_vma=False
    )
```

```python
import functools

import ml_dtypes
import numpy as np

import jax
import jax.numpy as jnp
from jax import lax
from jax.experimental import pallas as pl
from jax.experimental.pallas import tpu as pltpu
from jax.sharding import PartitionSpec as P

CHUNK = 8


def _expand_matrix(tile):
    rows = np.arange(tile)[:, None]
    cols = np.arange(8 * tile)[None, :]
    s = cols // tile
    j = cols % tile
    hit = rows == (tile // 8) * s + j // 8
    scale = (2.0 ** (7 - j % 8)).astype(np.float32)
    return np.where(hit, scale, 0.0).astype(ml_dtypes.bfloat16)


def _perm_matrix(tile):
    kk = tile // 8
    rows = np.arange(tile)[:, None]
    cols = np.arange(tile)[None, :]
    return rows == 8 * (cols % kk) + cols // kk


def _layer_kernel(cols_ref, counts_ref, grp_ref, adj_ref, xc_ref, deg_ref, w_ref, b_ref,
                  mexp_ref, perm_ref, pick_ref, *rest, per_tile, tile, n_table, n_grp, dev_blocks,
                  levels, per_dev):
    pieces = rest[:n_grp + 1]
    out_ref, table_ref, sems, words_ref, acc_ref = rest[n_grp + 1:]
    r = pl.program_id(0)
    count = counts_ref[r]
    g = grp_ref[0]
    me = grp_ref[1]
    part = n_grp * dev_blocks

    @pl.when(r == 0)
    def _():
        copies = []
        for d in range(n_grp):
            copies.append(pltpu.make_async_copy(
                pieces[d], table_ref.at[pl.ds(d * dev_blocks, dev_blocks)], sems.at[d]))
        n_halo = n_table - part
        copies.append(pltpu.make_async_copy(
            pieces[n_grp], table_ref.at[pl.ds(part, n_halo)], sems.at[n_grp]))
        for cp in copies:
            cp.start()
        for cp in copies:
            cp.wait()

    kk = tile // 8
    for k in range(kk):
        words_ref[pl.ds(k * per_tile, per_tile), :] = adj_ref[0, :, pl.ds(k * tile, tile)]
    acc_ref[...] = jnp.zeros_like(acc_ref)

    def chunk(c, masked):
            words = jnp.concatenate(
                [words_ref[pl.ds(c * CHUNK + tl, kk, stride=per_tile), :] for tl in range(CHUNK)],
                axis=0)
            spread = jnp.dot(words.astype(jnp.bfloat16), mexp_ref[...],
                             preferred_element_type=jnp.float32)
            bits = (spread.astype(jnp.int32) & 128).astype(jnp.bfloat16)
            rows = []
            for s in range(8):
                rows.append(jnp.concatenate(
                    [bits[tl * kk:(tl + 1) * kk, s * tile:(s + 1) * tile] for tl in range(CHUNK)],
                    axis=1))
            a_cat = jnp.concatenate(rows, axis=0)
            xs = []
            for tl in range(CHUNK):
                t = c * CHUNK + tl
                col = cols_ref[r, t]
                if n_grp == 4:
                    slot = jnp.bitwise_xor(col // dev_blocks, g)
                else:
                    slot = (g - col // dev_blocks + n_grp) % n_grp
                rel = slot * dev_blocks + col % dev_blocks
                h = jnp.maximum(col - part, 0)
                x = jnp.bitwise_xor(h // per_dev, me)
                pos = jnp.int32(0)
                for bit in range(levels):
                    pos = pos + ((x >> bit) & 1) * (1 << (levels - 1 - bit))
                hrel = part + pos * per_dev + h % per_dev
                col = jnp.clip(jnp.where(col < part, rel, hrel), 0, n_table - 1)
                xt = table_ref[col]
                if masked:
                    xt = jnp.where(t < count, xt, jnp.zeros_like(xt))
                xs.append(xt)
            x_cat = jnp.concatenate(xs, axis=0)
            acc_ref[...] += jnp.dot(a_cat, x_cat, preferred_element_type=jnp.float32)

    for c in range(per_tile // CHUNK):
        pl.when((c + 1) * CHUNK <= count)(functools.partial(chunk, c, False))
        pl.when((c * CHUNK < count) & (count < (c + 1) * CHUNK))(functools.partial(chunk, c, True))

    acc = acc_ref[...]
    totals = acc * (1.0 / 128.0)
    deg_row = deg_ref[pl.ds(r, 1), :].astype(jnp.float32)
    deg_perm = jnp.sum(pick_ref[...] * deg_row, axis=1, keepdims=True)
    avg_perm = (totals / deg_perm).astype(jnp.bfloat16)
    avg = jnp.dot(perm_ref[...], avg_perm, preferred_element_type=jnp.float32).astype(jnp.bfloat16)
    lhs = jnp.concatenate([xc_ref[...], avg], axis=1)
    summed = jnp.dot(lhs, w_ref[...], preferred_element_type=jnp.float32) + b_ref[...]
    out_ref[...] = jnp.maximum(summed, 0.0).astype(out_ref.dtype)


def on_device(
    x_current,
    x_cached,
    w_self,
    w_neigh,
    bias,
    tile_columns,
    tile_count,
    adjacency,
    degree,
    boundary_blocks,
):
    node_rows, width = x_current.shape
    row_blocks, per_tile = tile_columns.shape
    tile_rows = node_rows // row_blocks
    hidden = w_self.shape[1]
    kk = tile_rows // 8
    assert per_tile % CHUNK == 0
    n_grp = lax.psum(1, "grp")
    chosen = x_cached.reshape(row_blocks, tile_rows, width)[boundary_blocks[0]]
    n_dom = lax.psum(1, "dom")
    n_dev = n_dom * n_grp
    levels = n_dev.bit_length() - 1
    assert 1 << levels == n_dev
    me = lax.axis_index("dom") * n_grp + lax.axis_index("grp")
    halo_blocks = chosen
    for lv in range(levels):
        mask = n_dev >> (lv + 1)
        theirs = lax.ppermute(halo_blocks, ("dom", "grp"), [(i, i ^ mask) for i in range(n_dev)])
        halo_blocks = jnp.concatenate([halo_blocks, theirs], axis=0)
    own_blocks = x_current.reshape(row_blocks, tile_rows, width)
    pieces = [own_blocks]
    if n_grp == 4:
        near = lax.ppermute(own_blocks, "grp", [(i, i ^ 1) for i in range(4)])
        far = lax.ppermute(own_blocks, "grp", [(i, i ^ 2) for i in range(4)])
        far_near = lax.ppermute(far, "grp", [(i, i ^ 1) for i in range(4)])
        pieces += [near, far, far_near]
    else:
        for d in range(1, n_grp):
            pieces.append(lax.ppermute(own_blocks, "grp", [(i, (i + d) % n_grp) for i in range(n_grp)]))
    pieces.append(halo_blocks)
    n_table = n_grp * row_blocks + halo_blocks.shape[0]
    grp_idx = jnp.stack([lax.axis_index("grp"), me]).astype(jnp.int32)

    deg = degree.reshape(row_blocks, tile_rows)
    w_cat = jnp.concatenate([w_self, w_neigh], axis=0)
    b2 = bias.reshape(1, hidden)
    mexp = jnp.asarray(_expand_matrix(tile_rows))
    perm_np = _perm_matrix(tile_rows)
    perm = jnp.asarray(perm_np.astype(ml_dtypes.bfloat16))
    pick = jnp.asarray(perm_np.T.astype(np.float32))

    kernel = functools.partial(_layer_kernel, per_tile=per_tile, tile=tile_rows, n_table=n_table,
                               n_grp=n_grp, dev_blocks=row_blocks, levels=levels,
                               per_dev=chosen.shape[0])
    grid_spec = pltpu.PrefetchScalarGridSpec(
        num_scalar_prefetch=3,
        grid=(row_blocks,),
        in_specs=[
            pl.BlockSpec((1, per_tile, tile_rows * kk), lambda r, *_: (r, 0, 0)),
            pl.BlockSpec((tile_rows, width), lambda r, *_: (r, 0)),
            pl.BlockSpec((row_blocks, tile_rows), lambda r, *_: (0, 0)),
            pl.BlockSpec((2 * width, hidden), lambda r, *_: (0, 0)),
            pl.BlockSpec((1, hidden), lambda r, *_: (0, 0)),
            pl.BlockSpec((tile_rows, 8 * tile_rows), lambda r, *_: (0, 0)),
            pl.BlockSpec((tile_rows, tile_rows), lambda r, *_: (0, 0)),
            pl.BlockSpec((tile_rows, tile_rows), lambda r, *_: (0, 0)),
        ] + [pl.BlockSpec(memory_space=pl.ANY)] * (n_grp + 1),
        out_specs=pl.BlockSpec((tile_rows, hidden), lambda r, *_: (r, 0)),
        scratch_shapes=[pltpu.VMEM((n_table, tile_rows, width), jnp.bfloat16),
                        pltpu.SemaphoreType.DMA((n_grp + 1,)),
                        pltpu.VMEM((per_tile * kk, tile_rows), jnp.int32),
                        pltpu.VMEM((tile_rows, width), jnp.float32)],
    )
    return pl.pallas_call(
        kernel,
        grid_spec=grid_spec,
        out_shape=jax.ShapeDtypeStruct((node_rows, hidden), jnp.bfloat16),
        compiler_params=pltpu.CompilerParams(
            dimension_semantics=("arbitrary",), vmem_limit_bytes=48 * 1024 * 1024),
    )(tile_columns, tile_count, grp_idx, adjacency, x_current, deg, w_cat, b2, mexp, perm, pick, *pieces)


def solution(mesh):
    in_specs = (
        P(("dom", "grp"), None),
        P(("dom", "grp"), None),
        P(),
        P(),
        P(),
        P(("dom", "grp"), None),
        P(("dom", "grp")),
        P(("dom", "grp"), None, None),
        P(("dom", "grp")),
        P(("dom", "grp"), None),
    )
    out_specs = P(("dom", "grp"), None)
    return jax.shard_map(
        on_device, mesh=mesh, in_specs=in_specs, out_specs=out_specs, check_vma=False
    )
```

```python
import functools

import jax
import jax.numpy as jnp
from jax import lax
from jax.experimental import pallas as pl
from jax.experimental.pallas import tpu as pltpu
from jax.sharding import PartitionSpec as P

CHUNK = 8


def _layer_kernel(cols_ref, counts_ref, grp_ref, adj_ref, xc_ref, deg_ref, ws_ref, wn_ref, b_ref,
                  *rest, per_tile, tile, n_table, n_grp, dev_blocks,
                  levels, per_dev):
    pieces = rest[:n_grp + 1]
    out_ref, table_ref, sems, words_ref, acc_ref, mexp_ref, perm_ref, pick_ref = rest[n_grp + 1:]
    r = pl.program_id(0)
    count = counts_ref[r]
    g = grp_ref[0]
    me = grp_ref[1]
    part = n_grp * dev_blocks

    @pl.when(r == 0)
    def _():
        rows = lax.broadcasted_iota(jnp.int32, (tile, 8 * tile), 0)
        cols = lax.broadcasted_iota(jnp.int32, (tile, 8 * tile), 1)
        jj = cols % tile
        hit = rows == (tile // 8) * (cols // tile) + jj // 8
        scale = lax.shift_left(jnp.ones_like(jj), 7 - jj % 8).astype(jnp.float32)
        mexp_ref[...] = jnp.where(hit, scale, 0.0).astype(jnp.bfloat16)
        ri = lax.broadcasted_iota(jnp.int32, (tile, tile), 0)
        ci = lax.broadcasted_iota(jnp.int32, (tile, tile), 1)
        kq = tile // 8
        perm_ref[...] = (ri == 8 * (ci % kq) + ci // kq).astype(jnp.bfloat16)
        pick_ref[...] = (ci == 8 * (ri % kq) + ri // kq).astype(jnp.float32)
        copies = []
        for d in range(n_grp):
            copies.append(pltpu.make_async_copy(
                pieces[d], table_ref.at[pl.ds(d * dev_blocks, dev_blocks)], sems.at[d]))
        n_halo = n_table - part
        copies.append(pltpu.make_async_copy(
            pieces[n_grp], table_ref.at[pl.ds(part, n_halo)], sems.at[n_grp]))
        for cp in copies:
            cp.start()
        for cp in copies:
            cp.wait()

    kk = tile // 8
    for k in range(kk):
        words_ref[pl.ds(k * per_tile, per_tile), :] = adj_ref[0, :, pl.ds(k * tile, tile)]
    acc_ref[...] = jnp.zeros_like(acc_ref)

    def chunk(c, masked):
            words = jnp.concatenate(
                [words_ref[pl.ds(c * CHUNK + tl, kk, stride=per_tile), :] for tl in range(CHUNK)],
                axis=0)
            spread = jnp.dot(words.astype(jnp.bfloat16), mexp_ref[...],
                             preferred_element_type=jnp.float32)
            bits = (spread.astype(jnp.int32) & 128).astype(jnp.bfloat16)
            rows = []
            for s in range(8):
                rows.append(jnp.concatenate(
                    [bits[tl * kk:(tl + 1) * kk, s * tile:(s + 1) * tile] for tl in range(CHUNK)],
                    axis=1))
            a_cat = jnp.concatenate(rows, axis=0)
            xs = []
            for tl in range(CHUNK):
                t = c * CHUNK + tl
                col = cols_ref[r, t]
                if n_grp == 4:
                    slot = jnp.bitwise_xor(col // dev_blocks, g)
                else:
                    slot = (g - col // dev_blocks + n_grp) % n_grp
                rel = slot * dev_blocks + col % dev_blocks
                h = jnp.maximum(col - part, 0)
                x = jnp.bitwise_xor(h // per_dev, me)
                pos = jnp.int32(0)
                for bit in range(levels):
                    pos = pos + ((x >> bit) & 1) * (1 << (levels - 1 - bit))
                hrel = part + pos * per_dev + h % per_dev
                col = jnp.clip(jnp.where(col < part, rel, hrel), 0, n_table - 1)
                xt = table_ref[col]
                if masked:
                    xt = jnp.where(t < count, xt, jnp.zeros_like(xt))
                xs.append(xt)
            x_cat = jnp.concatenate(xs, axis=0)
            acc_ref[...] += jnp.dot(a_cat, x_cat, preferred_element_type=jnp.float32)

    for c in range(per_tile // CHUNK):
        pl.when((c + 1) * CHUNK <= count)(functools.partial(chunk, c, False))
        pl.when((c * CHUNK < count) & (count < (c + 1) * CHUNK))(functools.partial(chunk, c, True))

    acc = acc_ref[...]
    totals = acc * (1.0 / 128.0)
    deg_row = deg_ref[pl.ds(r, 1), :].astype(jnp.float32)
    deg_perm = jnp.sum(pick_ref[...] * deg_row, axis=1, keepdims=True)
    avg_perm = (totals / deg_perm).astype(jnp.bfloat16)
    avg = jnp.dot(perm_ref[...], avg_perm, preferred_element_type=jnp.float32).astype(jnp.bfloat16)
    summed = (jnp.dot(xc_ref[...], ws_ref[...], preferred_element_type=jnp.float32)
              + jnp.dot(avg, wn_ref[...], preferred_element_type=jnp.float32) + b_ref[...])
    out_ref[...] = jnp.maximum(summed, 0.0).astype(out_ref.dtype)


def on_device(
    x_current,
    x_cached,
    w_self,
    w_neigh,
    bias,
    tile_columns,
    tile_count,
    adjacency,
    degree,
    boundary_blocks,
):
    node_rows, width = x_current.shape
    row_blocks, per_tile = tile_columns.shape
    tile_rows = node_rows // row_blocks
    hidden = w_self.shape[1]
    kk = tile_rows // 8
    assert per_tile % CHUNK == 0
    n_grp = lax.psum(1, "grp")
    chosen = x_cached.reshape(row_blocks, tile_rows, width)[boundary_blocks[0]]
    n_dom = lax.psum(1, "dom")
    n_dev = n_dom * n_grp
    levels = n_dev.bit_length() - 1
    assert 1 << levels == n_dev
    me = lax.axis_index("dom") * n_grp + lax.axis_index("grp")
    halo_blocks = chosen
    for lv in range(levels):
        mask = n_dev >> (lv + 1)
        theirs = lax.ppermute(halo_blocks, ("dom", "grp"), [(i, i ^ mask) for i in range(n_dev)])
        halo_blocks = jnp.concatenate([halo_blocks, theirs], axis=0)
    own_blocks = x_current.reshape(row_blocks, tile_rows, width)
    pieces = [own_blocks]
    if n_grp == 4:
        near = lax.ppermute(own_blocks, "grp", [(i, i ^ 1) for i in range(4)])
        far = lax.ppermute(own_blocks, "grp", [(i, i ^ 2) for i in range(4)])
        far_near = lax.ppermute(far, "grp", [(i, i ^ 1) for i in range(4)])
        pieces += [near, far, far_near]
    else:
        for d in range(1, n_grp):
            pieces.append(lax.ppermute(own_blocks, "grp", [(i, (i + d) % n_grp) for i in range(n_grp)]))
    pieces.append(halo_blocks)
    n_table = n_grp * row_blocks + halo_blocks.shape[0]
    grp_idx = jnp.stack([lax.axis_index("grp"), me]).astype(jnp.int32)

    deg = degree.reshape(row_blocks, tile_rows)
    b2 = bias.reshape(1, hidden)

    kernel = functools.partial(_layer_kernel, per_tile=per_tile, tile=tile_rows, n_table=n_table,
                               n_grp=n_grp, dev_blocks=row_blocks, levels=levels,
                               per_dev=chosen.shape[0])
    grid_spec = pltpu.PrefetchScalarGridSpec(
        num_scalar_prefetch=3,
        grid=(row_blocks,),
        in_specs=[
            pl.BlockSpec((1, per_tile, tile_rows * kk), lambda r, *_: (r, 0, 0)),
            pl.BlockSpec((tile_rows, width), lambda r, *_: (r, 0)),
            pl.BlockSpec((row_blocks, tile_rows), lambda r, *_: (0, 0)),
            pl.BlockSpec((width, hidden), lambda r, *_: (0, 0)),
            pl.BlockSpec((width, hidden), lambda r, *_: (0, 0)),
            pl.BlockSpec((1, hidden), lambda r, *_: (0, 0)),
        ] + [pl.BlockSpec(memory_space=pl.ANY)] * (n_grp + 1),
        out_specs=pl.BlockSpec((tile_rows, hidden), lambda r, *_: (r, 0)),
        scratch_shapes=[pltpu.VMEM((n_table, tile_rows, width), jnp.bfloat16),
                        pltpu.SemaphoreType.DMA((n_grp + 1,)),
                        pltpu.VMEM((per_tile * kk, tile_rows), jnp.int32),
                        pltpu.VMEM((tile_rows, width), jnp.float32),
                        pltpu.VMEM((tile_rows, 8 * tile_rows), jnp.bfloat16),
                        pltpu.VMEM((tile_rows, tile_rows), jnp.bfloat16),
                        pltpu.VMEM((tile_rows, tile_rows), jnp.float32)],
    )
    return pl.pallas_call(
        kernel,
        grid_spec=grid_spec,
        out_shape=jax.ShapeDtypeStruct((node_rows, hidden), jnp.bfloat16),
        compiler_params=pltpu.CompilerParams(
            dimension_semantics=("arbitrary",), vmem_limit_bytes=48 * 1024 * 1024),
    )(tile_columns, tile_count, grp_idx, adjacency, x_current, deg, w_self, w_neigh, b2, *pieces)


def solution(mesh):
    in_specs = (
        P(("dom", "grp"), None),
        P(("dom", "grp"), None),
        P(),
        P(),
        P(),
        P(("dom", "grp"), None),
        P(("dom", "grp")),
        P(("dom", "grp"), None, None),
        P(("dom", "grp")),
        P(("dom", "grp"), None),
    )
    out_specs = P(("dom", "grp"), None)
    return jax.shard_map(
        on_device, mesh=mesh, in_specs=in_specs, out_specs=out_specs, check_vma=False
    )
```

```python
import functools

import jax
import jax.numpy as jnp
from jax import lax
from jax.experimental import pallas as pl
from jax.experimental.pallas import tpu as pltpu
from jax.sharding import PartitionSpec as P

CHUNK = 8


def _layer_kernel(cols_ref, counts_ref, grp_ref, adj_ref, xc_ref, deg_ref, ws_ref, wn_ref, b_ref,
                  *rest, per_tile, tile, n_table, n_grp, dev_blocks,
                  levels, per_dev):
    pieces = rest[:n_grp + 1]
    out_ref, table_ref, sems, words_ref, acc_ref, mexp_ref, perm_ref, pick_ref = rest[n_grp + 1:]
    r = pl.program_id(0)
    count = counts_ref[r]
    g = grp_ref[0]
    me = grp_ref[1]
    part = n_grp * dev_blocks

    @pl.when(r == 0)
    def _():
        rows = lax.broadcasted_iota(jnp.int32, (tile, 8 * tile), 0)
        cols = lax.broadcasted_iota(jnp.int32, (tile, 8 * tile), 1)
        jj = cols % tile
        hit = rows == (tile // 8) * (cols // tile) + jj // 8
        scale = lax.shift_left(jnp.ones_like(jj), 7 - jj % 8).astype(jnp.float32)
        mexp_ref[...] = jnp.where(hit, scale, 0.0).astype(jnp.bfloat16)
        ri = lax.broadcasted_iota(jnp.int32, (tile, tile), 0)
        ci = lax.broadcasted_iota(jnp.int32, (tile, tile), 1)
        kq = tile // 8
        perm_ref[...] = (ri == 8 * (ci % kq) + ci // kq).astype(jnp.bfloat16)
        pick_ref[...] = (ci == 8 * (ri % kq) + ri // kq).astype(jnp.float32)
        copies = []
        for d in range(n_grp):
            copies.append(pltpu.make_async_copy(
                pieces[d], table_ref.at[pl.ds(d * dev_blocks, dev_blocks)], sems.at[d]))
        n_halo = n_table - part
        copies.append(pltpu.make_async_copy(
            pieces[n_grp], table_ref.at[pl.ds(part, n_halo)], sems.at[n_grp]))
        for cp in copies:
            cp.start()
        for cp in copies:
            cp.wait()

    kk = tile // 8
    for k in range(kk):
        words_ref[pl.ds(k * per_tile, per_tile), :] = adj_ref[0, :, pl.ds(k * tile, tile)]
    acc_ref[...] = jnp.zeros_like(acc_ref)

    def chunk(c, masked):
            words = jnp.concatenate(
                [words_ref[pl.ds(c * CHUNK + tl, kk, stride=per_tile), :] for tl in range(CHUNK)],
                axis=0)
            spread = jnp.dot(words.astype(jnp.bfloat16), mexp_ref[...],
                             preferred_element_type=jnp.float32)
            bits = (spread.astype(jnp.int32) & 128).astype(jnp.bfloat16)
            rows = []
            for s in range(8):
                rows.append(jnp.concatenate(
                    [bits[tl * kk:(tl + 1) * kk, s * tile:(s + 1) * tile] for tl in range(CHUNK)],
                    axis=1))
            a_cat = jnp.concatenate(rows, axis=0)
            xs = []
            for tl in range(CHUNK):
                t = c * CHUNK + tl
                col = cols_ref[r, t]
                if n_grp == 4:
                    slot = jnp.bitwise_xor(col // dev_blocks, g)
                else:
                    slot = (g - col // dev_blocks + n_grp) % n_grp
                rel = slot * dev_blocks + col % dev_blocks
                h = jnp.maximum(col - part, 0)
                x = jnp.bitwise_xor(h // per_dev, me)
                pos = jnp.int32(0)
                for bit in range(levels):
                    pos = pos + ((x >> bit) & 1) * (1 << (levels - 1 - bit))
                hrel = part + pos * per_dev + h % per_dev
                col = jnp.clip(jnp.where(col < part, rel, hrel), 0, n_table - 1)
                xt = table_ref[col]
                if masked:
                    xt = jnp.where(t < count, xt, jnp.zeros_like(xt))
                xs.append(xt)
            x_cat = jnp.concatenate(xs, axis=0)
            acc_ref[...] += jnp.dot(a_cat, x_cat, preferred_element_type=jnp.float32)

    for c in range(per_tile // CHUNK):
        pl.when((c + 1) * CHUNK <= count)(functools.partial(chunk, c, False))
        pl.when((c * CHUNK < count) & (count < (c + 1) * CHUNK))(functools.partial(chunk, c, True))

    acc = acc_ref[...]
    totals = acc * (1.0 / 128.0)
    deg_row = deg_ref[pl.ds(r, 1), :].astype(jnp.float32)
    deg_perm = jnp.sum(pick_ref[...] * deg_row, axis=1, keepdims=True)
    avg_perm = (totals / deg_perm).astype(jnp.bfloat16)
    avg = jnp.dot(perm_ref[...], avg_perm, preferred_element_type=jnp.float32).astype(jnp.bfloat16)
    summed = (jnp.dot(xc_ref[...], ws_ref[...], preferred_element_type=jnp.float32)
              + jnp.dot(avg, wn_ref[...], preferred_element_type=jnp.float32) + b_ref[...])
    out_ref[...] = jnp.maximum(summed, 0.0).astype(out_ref.dtype)


def on_device(
    x_current,
    x_cached,
    w_self,
    w_neigh,
    bias,
    tile_columns,
    tile_count,
    adjacency,
    degree,
    boundary_blocks,
):
    node_rows, width = x_current.shape
    row_blocks, per_tile = tile_columns.shape
    tile_rows = node_rows // row_blocks
    hidden = w_self.shape[1]
    kk = tile_rows // 8
    assert per_tile % CHUNK == 0
    n_grp = lax.psum(1, "grp")
    chosen = x_cached.reshape(row_blocks, tile_rows, width)[boundary_blocks[0]]
    n_dom = lax.psum(1, "dom")
    n_dev = n_dom * n_grp
    levels = n_dev.bit_length() - 1
    assert 1 << levels == n_dev
    me = lax.axis_index("dom") * n_grp + lax.axis_index("grp")
    halo_blocks = chosen
    for lv in range(levels):
        mask = n_dev >> (lv + 1)
        theirs = lax.ppermute(halo_blocks, ("dom", "grp"), [(i, i ^ mask) for i in range(n_dev)])
        halo_blocks = jnp.concatenate([halo_blocks, theirs], axis=0)
    own_blocks = x_current.reshape(row_blocks, tile_rows, width)
    pieces = [own_blocks]
    if n_grp == 4:
        near = lax.ppermute(own_blocks, "grp", [(i, i ^ 1) for i in range(4)])
        far = lax.ppermute(own_blocks, "grp", [(i, i ^ 2) for i in range(4)])
        far_near = lax.ppermute(far, "grp", [(i, i ^ 1) for i in range(4)])
        pieces += [near, far, far_near]
    else:
        for d in range(1, n_grp):
            pieces.append(lax.ppermute(own_blocks, "grp", [(i, (i + d) % n_grp) for i in range(n_grp)]))
    pieces.append(halo_blocks)
    n_table = n_grp * row_blocks + halo_blocks.shape[0]
    grp_idx = jnp.stack([lax.axis_index("grp"), me]).astype(jnp.int32)

    deg = degree.reshape(row_blocks, tile_rows)
    b2 = bias.reshape(1, hidden)

    kernel = functools.partial(_layer_kernel, per_tile=per_tile, tile=tile_rows, n_table=n_table,
                               n_grp=n_grp, dev_blocks=row_blocks, levels=levels,
                               per_dev=chosen.shape[0])
    grid_spec = pltpu.PrefetchScalarGridSpec(
        num_scalar_prefetch=3,
        grid=(row_blocks,),
        in_specs=[
            pl.BlockSpec((1, per_tile, tile_rows * kk), lambda r, *_: (r, 0, 0)),
            pl.BlockSpec((tile_rows, width), lambda r, *_: (r, 0)),
            pl.BlockSpec((row_blocks, tile_rows), lambda r, *_: (0, 0)),
            pl.BlockSpec((width, hidden), lambda r, *_: (0, 0)),
            pl.BlockSpec((width, hidden), lambda r, *_: (0, 0)),
            pl.BlockSpec((1, hidden), lambda r, *_: (0, 0)),
        ] + [pl.BlockSpec(memory_space=pl.ANY)] * (n_grp + 1),
        out_specs=pl.BlockSpec((tile_rows, hidden), lambda r, *_: (r, 0)),
        scratch_shapes=[pltpu.VMEM((n_table, tile_rows, width), jnp.bfloat16),
                        pltpu.SemaphoreType.DMA((n_grp + 1,)),
                        pltpu.VMEM((per_tile * kk, tile_rows), jnp.int32),
                        pltpu.VMEM((tile_rows, width), jnp.float32),
                        pltpu.VMEM((tile_rows, 8 * tile_rows), jnp.bfloat16),
                        pltpu.VMEM((tile_rows, tile_rows), jnp.bfloat16),
                        pltpu.VMEM((tile_rows, tile_rows), jnp.float32)],
    )
    return pl.pallas_call(
        kernel,
        grid_spec=grid_spec,
        out_shape=jax.ShapeDtypeStruct((node_rows, hidden), jnp.bfloat16),
        compiler_params=pltpu.CompilerParams(
            dimension_semantics=("arbitrary",), vmem_limit_bytes=48 * 1024 * 1024),
    )(*[pltpu.with_memory_space_constraint(a, pltpu.HBM) for a in
        (tile_columns, tile_count, grp_idx, adjacency, x_current, deg, w_self, w_neigh, b2)], *pieces)


def solution(mesh):
    in_specs = (
        P(("dom", "grp"), None),
        P(("dom", "grp"), None),
        P(),
        P(),
        P(),
        P(("dom", "grp"), None),
        P(("dom", "grp")),
        P(("dom", "grp"), None, None),
        P(("dom", "grp")),
        P(("dom", "grp"), None),
    )
    out_specs = P(("dom", "grp"), None)
    return jax.shard_map(
        on_device, mesh=mesh, in_specs=in_specs, out_specs=out_specs, check_vma=False
    )
```

```python
import functools

import jax
import jax.numpy as jnp
from jax import lax
from jax.experimental import pallas as pl
from jax.experimental.pallas import tpu as pltpu
from jax.sharding import PartitionSpec as P

CHUNK = 8


def _layer_kernel(cols_ref, counts_ref, grp_ref, adj_ref, xc_ref, deg_ref, ws_ref, wn_ref, b_ref,
                  *rest, per_tile, tile, n_table, n_grp, dev_blocks):
    pieces = rest[:n_grp + 1]
    out_ref, table_ref, sems, words_ref, acc_ref, mexp_ref, perm_ref, pick_ref = rest[n_grp + 1:]
    r = pl.program_id(0)
    count = counts_ref[r]
    g = grp_ref[0]
    part = n_grp * dev_blocks

    @pl.when(r == 0)
    def _():
        rows = lax.broadcasted_iota(jnp.int32, (tile, 8 * tile), 0)
        cols = lax.broadcasted_iota(jnp.int32, (tile, 8 * tile), 1)
        jj = cols % tile
        hit = rows == (tile // 8) * (cols // tile) + jj // 8
        scale = lax.shift_left(jnp.ones_like(jj), 7 - jj % 8).astype(jnp.float32)
        mexp_ref[...] = jnp.where(hit, scale, 0.0).astype(jnp.bfloat16)
        ri = lax.broadcasted_iota(jnp.int32, (tile, tile), 0)
        ci = lax.broadcasted_iota(jnp.int32, (tile, tile), 1)
        kq = tile // 8
        perm_ref[...] = (ri == 8 * (ci % kq) + ci // kq).astype(jnp.bfloat16)
        pick_ref[...] = (ci == 8 * (ri % kq) + ri // kq).astype(jnp.float32)
        copies = []
        for d in range(n_grp):
            copies.append(pltpu.make_async_copy(
                pieces[d], table_ref.at[pl.ds(d * dev_blocks, dev_blocks)], sems.at[d]))
        n_halo = n_table - part
        copies.append(pltpu.make_async_copy(
            pieces[n_grp], table_ref.at[pl.ds(part, n_halo)], sems.at[n_grp]))
        for cp in copies:
            cp.start()
        for cp in copies:
            cp.wait()

    kk = tile // 8
    for k in range(kk):
        words_ref[pl.ds(k * per_tile, per_tile), :] = adj_ref[0, :, pl.ds(k * tile, tile)]
    acc_ref[...] = jnp.zeros_like(acc_ref)

    def chunk(c, masked):
            words = jnp.concatenate(
                [words_ref[pl.ds(c * CHUNK + tl, kk, stride=per_tile), :] for tl in range(CHUNK)],
                axis=0)
            spread = jnp.dot(words.astype(jnp.bfloat16), mexp_ref[...],
                             preferred_element_type=jnp.float32)
            bits = (spread.astype(jnp.int32) & 128).astype(jnp.bfloat16)
            rows = []
            for s in range(8):
                rows.append(jnp.concatenate(
                    [bits[tl * kk:(tl + 1) * kk, s * tile:(s + 1) * tile] for tl in range(CHUNK)],
                    axis=1))
            a_cat = jnp.concatenate(rows, axis=0)
            xs = []
            for tl in range(CHUNK):
                t = c * CHUNK + tl
                col = cols_ref[r, t]
                if n_grp == 4:
                    slot = jnp.bitwise_xor(col // dev_blocks, g)
                else:
                    slot = (g - col // dev_blocks + n_grp) % n_grp
                rel = slot * dev_blocks + col % dev_blocks
                col = jnp.clip(jnp.where(col < part, rel, col), 0, n_table - 1)
                xt = table_ref[col]
                if masked:
                    xt = jnp.where(t < count, xt, jnp.zeros_like(xt))
                xs.append(xt)
            x_cat = jnp.concatenate(xs, axis=0)
            acc_ref[...] += jnp.dot(a_cat, x_cat, preferred_element_type=jnp.float32)

    for c in range(per_tile // CHUNK):
        pl.when((c + 1) * CHUNK <= count)(functools.partial(chunk, c, False))
        pl.when((c * CHUNK < count) & (count < (c + 1) * CHUNK))(functools.partial(chunk, c, True))

    acc = acc_ref[...]
    totals = acc * (1.0 / 128.0)
    deg_row = deg_ref[pl.ds(r, 1), :].astype(jnp.float32)
    deg_perm = jnp.sum(pick_ref[...] * deg_row, axis=1, keepdims=True)
    avg_perm = (totals / deg_perm).astype(jnp.bfloat16)
    avg = jnp.dot(perm_ref[...], avg_perm, preferred_element_type=jnp.float32).astype(jnp.bfloat16)
    summed = (jnp.dot(xc_ref[...], ws_ref[...], preferred_element_type=jnp.float32)
              + jnp.dot(avg, wn_ref[...], preferred_element_type=jnp.float32) + b_ref[...])
    out_ref[...] = jnp.maximum(summed, 0.0).astype(out_ref.dtype)


def on_device(
    x_current,
    x_cached,
    w_self,
    w_neigh,
    bias,
    tile_columns,
    tile_count,
    adjacency,
    degree,
    boundary_blocks,
):
    node_rows, width = x_current.shape
    row_blocks, per_tile = tile_columns.shape
    tile_rows = node_rows // row_blocks
    hidden = w_self.shape[1]
    kk = tile_rows // 8
    assert per_tile % CHUNK == 0
    n_grp = lax.psum(1, "grp")
    chosen = x_cached.reshape(row_blocks, tile_rows, width)[boundary_blocks[0]]
    n_dom = lax.psum(1, "dom")
    n_dev = n_dom * n_grp
    spread_out = jnp.broadcast_to(chosen[None], (n_dev,) + chosen.shape).reshape(
        (n_dev * chosen.shape[0],) + chosen.shape[1:])
    halo_blocks = lax.all_to_all(spread_out, ("dom", "grp"), 0, 0, tiled=True)
    own_blocks = x_current.reshape(row_blocks, tile_rows, width)
    pieces = [own_blocks]
    if n_grp == 4:
        near = lax.ppermute(own_blocks, "grp", [(i, i ^ 1) for i in range(4)])
        far = lax.ppermute(own_blocks, "grp", [(i, i ^ 2) for i in range(4)])
        far_near = lax.ppermute(far, "grp", [(i, i ^ 1) for i in range(4)])
        pieces += [near, far, far_near]
    else:
        for d in range(1, n_grp):
            pieces.append(lax.ppermute(own_blocks, "grp", [(i, (i + d) % n_grp) for i in range(n_grp)]))
    pieces.append(halo_blocks)
    n_table = n_grp * row_blocks + halo_blocks.shape[0]
    grp_idx = jnp.stack([lax.axis_index("grp"), lax.axis_index("grp")]).astype(jnp.int32)

    deg = degree.reshape(row_blocks, tile_rows)
    b2 = bias.reshape(1, hidden)

    kernel = functools.partial(_layer_kernel, per_tile=per_tile, tile=tile_rows, n_table=n_table,
                               n_grp=n_grp, dev_blocks=row_blocks)
    grid_spec = pltpu.PrefetchScalarGridSpec(
        num_scalar_prefetch=3,
        grid=(row_blocks,),
        in_specs=[
            pl.BlockSpec((1, per_tile, tile_rows * kk), lambda r, *_: (r, 0, 0)),
            pl.BlockSpec((tile_rows, width), lambda r, *_: (r, 0)),
            pl.BlockSpec((row_blocks, tile_rows), lambda r, *_: (0, 0)),
            pl.BlockSpec((width, hidden), lambda r, *_: (0, 0)),
            pl.BlockSpec((width, hidden), lambda r, *_: (0, 0)),
            pl.BlockSpec((1, hidden), lambda r, *_: (0, 0)),
        ] + [pl.BlockSpec(memory_space=pl.ANY)] * (n_grp + 1),
        out_specs=pl.BlockSpec((tile_rows, hidden), lambda r, *_: (r, 0)),
        scratch_shapes=[pltpu.VMEM((n_table, tile_rows, width), jnp.bfloat16),
                        pltpu.SemaphoreType.DMA((n_grp + 1,)),
                        pltpu.VMEM((per_tile * kk, tile_rows), jnp.int32),
                        pltpu.VMEM((tile_rows, width), jnp.float32),
                        pltpu.VMEM((tile_rows, 8 * tile_rows), jnp.bfloat16),
                        pltpu.VMEM((tile_rows, tile_rows), jnp.bfloat16),
                        pltpu.VMEM((tile_rows, tile_rows), jnp.float32)],
    )
    return pl.pallas_call(
        kernel,
        grid_spec=grid_spec,
        out_shape=jax.ShapeDtypeStruct((node_rows, hidden), jnp.bfloat16),
        compiler_params=pltpu.CompilerParams(
            dimension_semantics=("arbitrary",), vmem_limit_bytes=48 * 1024 * 1024),
    )(*[pltpu.with_memory_space_constraint(a, pltpu.HBM) for a in
        (tile_columns, tile_count, grp_idx, adjacency, x_current, deg, w_self, w_neigh, b2)], *pieces)


def solution(mesh):
    in_specs = (
        P(("dom", "grp"), None),
        P(("dom", "grp"), None),
        P(),
        P(),
        P(),
        P(("dom", "grp"), None),
        P(("dom", "grp")),
        P(("dom", "grp"), None, None),
        P(("dom", "grp")),
        P(("dom", "grp"), None),
    )
    out_specs = P(("dom", "grp"), None)
    return jax.shard_map(
        on_device, mesh=mesh, in_specs=in_specs, out_specs=out_specs, check_vma=False
    )
```

```python
import functools

import jax
import jax.numpy as jnp
from jax import lax
from jax.experimental import pallas as pl
from jax.experimental.pallas import tpu as pltpu
from jax.sharding import PartitionSpec as P

CHUNK = 8


def _layer_kernel(cols_ref, counts_ref, grp_ref, adj_ref, xc_ref, deg_ref, ws_ref, wn_ref, b_ref,
                  *rest, per_tile, tile, n_table, n_grp, dev_blocks,
                  offsets):
    n_pieces = len(offsets)
    pieces = rest[:n_pieces]
    out_ref, table_ref, sems, words_ref, acc_ref, mexp_ref, perm_ref, pick_ref = rest[n_pieces:]
    r = pl.program_id(0)
    count = counts_ref[r]
    g = grp_ref[0]
    part = n_grp * dev_blocks

    @pl.when(r == 0)
    def _():
        rows = lax.broadcasted_iota(jnp.int32, (tile, 8 * tile), 0)
        cols = lax.broadcasted_iota(jnp.int32, (tile, 8 * tile), 1)
        jj = cols % tile
        hit = rows == (tile // 8) * (cols // tile) + jj // 8
        scale = lax.shift_left(jnp.ones_like(jj), 7 - jj % 8).astype(jnp.float32)
        mexp_ref[...] = jnp.where(hit, scale, 0.0).astype(jnp.bfloat16)
        ri = lax.broadcasted_iota(jnp.int32, (tile, tile), 0)
        ci = lax.broadcasted_iota(jnp.int32, (tile, tile), 1)
        kq = tile // 8
        perm_ref[...] = (ri == 8 * (ci % kq) + ci // kq).astype(jnp.bfloat16)
        pick_ref[...] = (ci == 8 * (ri % kq) + ri // kq).astype(jnp.float32)
        copies = []
        for d in range(n_pieces):
            copies.append(pltpu.make_async_copy(
                pieces[d], table_ref.at[pl.ds(offsets[d], pieces[d].shape[0])], sems.at[d]))
        for cp in copies:
            cp.start()
        for cp in copies:
            cp.wait()

    kk = tile // 8
    for k in range(kk):
        words_ref[pl.ds(k * per_tile, per_tile), :] = adj_ref[0, :, pl.ds(k * tile, tile)]
    acc_ref[...] = jnp.zeros_like(acc_ref)

    def chunk(c, masked):
            words = jnp.concatenate(
                [words_ref[pl.ds(c * CHUNK + tl, kk, stride=per_tile), :] for tl in range(CHUNK)],
                axis=0)
            spread = jnp.dot(words.astype(jnp.bfloat16), mexp_ref[...],
                             preferred_element_type=jnp.float32)
            bits = (spread.astype(jnp.int32) & 128).astype(jnp.bfloat16)
            rows = []
            for s in range(8):
                rows.append(jnp.concatenate(
                    [bits[tl * kk:(tl + 1) * kk, s * tile:(s + 1) * tile] for tl in range(CHUNK)],
                    axis=1))
            a_cat = jnp.concatenate(rows, axis=0)
            xs = []
            for tl in range(CHUNK):
                t = c * CHUNK + tl
                col = cols_ref[r, t]
                if n_grp == 4:
                    slot = jnp.bitwise_xor(col // dev_blocks, g)
                else:
                    slot = (g - col // dev_blocks + n_grp) % n_grp
                rel = slot * dev_blocks + col % dev_blocks
                col = jnp.clip(jnp.where(col < part, rel, col), 0, n_table - 1)
                xt = table_ref[col]
                if masked:
                    xt = jnp.where(t < count, xt, jnp.zeros_like(xt))
                xs.append(xt)
            x_cat = jnp.concatenate(xs, axis=0)
            acc_ref[...] += jnp.dot(a_cat, x_cat, preferred_element_type=jnp.float32)

    for c in range(per_tile // CHUNK):
        pl.when((c + 1) * CHUNK <= count)(functools.partial(chunk, c, False))
        pl.when((c * CHUNK < count) & (count < (c + 1) * CHUNK))(functools.partial(chunk, c, True))

    acc = acc_ref[...]
    totals = acc * (1.0 / 128.0)
    deg_row = deg_ref[pl.ds(r, 1), :].astype(jnp.float32)
    deg_perm = jnp.sum(pick_ref[...] * deg_row, axis=1, keepdims=True)
    avg_perm = (totals / deg_perm).astype(jnp.bfloat16)
    avg = jnp.dot(perm_ref[...], avg_perm, preferred_element_type=jnp.float32).astype(jnp.bfloat16)
    summed = (jnp.dot(xc_ref[...], ws_ref[...], preferred_element_type=jnp.float32)
              + jnp.dot(avg, wn_ref[...], preferred_element_type=jnp.float32) + b_ref[...])
    out_ref[...] = jnp.maximum(summed, 0.0).astype(out_ref.dtype)


def on_device(
    x_current,
    x_cached,
    w_self,
    w_neigh,
    bias,
    tile_columns,
    tile_count,
    adjacency,
    degree,
    boundary_blocks,
):
    node_rows, width = x_current.shape
    row_blocks, per_tile = tile_columns.shape
    tile_rows = node_rows // row_blocks
    hidden = w_self.shape[1]
    kk = tile_rows // 8
    assert per_tile % CHUNK == 0
    n_grp = lax.psum(1, "grp")
    chosen = x_cached.reshape(row_blocks, tile_rows, width)[boundary_blocks[0]]
    n_dom = lax.psum(1, "dom")
    n_dev = n_dom * n_grp
    spread_out = jnp.broadcast_to(chosen[None], (n_dev,) + chosen.shape).reshape(
        (n_dev * chosen.shape[0],) + chosen.shape[1:])
    halo_blocks = lax.all_to_all(spread_out, ("dom", "grp"), 0, 0, tiled=True)
    own_blocks = x_current.reshape(row_blocks, tile_rows, width)
    pieces = [own_blocks]
    offsets = [0]
    if n_grp == 4:
        half = row_blocks // 2
        near = lax.ppermute(own_blocks, "grp", [(i, i ^ 1) for i in range(4)])
        far = [lax.ppermute(own_blocks[a:b], "grp", [(i, i ^ 2) for i in range(4)])
               for a, b in ((0, half), (half, row_blocks))]
        far_near = [lax.ppermute(f, "grp", [(i, i ^ 1) for i in range(4)]) for f in far]
        pieces += [near] + far + far_near
        offsets += [row_blocks, 2 * row_blocks, 2 * row_blocks + half,
                    3 * row_blocks, 3 * row_blocks + half]
    else:
        for d in range(1, n_grp):
            pieces.append(lax.ppermute(own_blocks, "grp", [(i, (i + d) % n_grp) for i in range(n_grp)]))
            offsets.append(d * row_blocks)
    offsets.append(n_grp * row_blocks)
    pieces.append(halo_blocks)
    n_table = n_grp * row_blocks + halo_blocks.shape[0]
    grp_idx = jnp.stack([lax.axis_index("grp"), lax.axis_index("grp")]).astype(jnp.int32)

    deg = degree.reshape(row_blocks, tile_rows)
    b2 = bias.reshape(1, hidden)

    kernel = functools.partial(_layer_kernel, per_tile=per_tile, tile=tile_rows, n_table=n_table,
                               n_grp=n_grp, dev_blocks=row_blocks, offsets=tuple(offsets))
    grid_spec = pltpu.PrefetchScalarGridSpec(
        num_scalar_prefetch=3,
        grid=(row_blocks,),
        in_specs=[
            pl.BlockSpec((1, per_tile, tile_rows * kk), lambda r, *_: (r, 0, 0)),
            pl.BlockSpec((tile_rows, width), lambda r, *_: (r, 0)),
            pl.BlockSpec((row_blocks, tile_rows), lambda r, *_: (0, 0)),
            pl.BlockSpec((width, hidden), lambda r, *_: (0, 0)),
            pl.BlockSpec((width, hidden), lambda r, *_: (0, 0)),
            pl.BlockSpec((1, hidden), lambda r, *_: (0, 0)),
        ] + [pl.BlockSpec(memory_space=pl.ANY)] * len(pieces),
        out_specs=pl.BlockSpec((tile_rows, hidden), lambda r, *_: (r, 0)),
        scratch_shapes=[pltpu.VMEM((n_table, tile_rows, width), jnp.bfloat16),
                        pltpu.SemaphoreType.DMA((len(pieces),)),
                        pltpu.VMEM((per_tile * kk, tile_rows), jnp.int32),
                        pltpu.VMEM((tile_rows, width), jnp.float32),
                        pltpu.VMEM((tile_rows, 8 * tile_rows), jnp.bfloat16),
                        pltpu.VMEM((tile_rows, tile_rows), jnp.bfloat16),
                        pltpu.VMEM((tile_rows, tile_rows), jnp.float32)],
    )
    return pl.pallas_call(
        kernel,
        grid_spec=grid_spec,
        out_shape=jax.ShapeDtypeStruct((node_rows, hidden), jnp.bfloat16),
        compiler_params=pltpu.CompilerParams(
            dimension_semantics=("arbitrary",), vmem_limit_bytes=48 * 1024 * 1024),
    )(*[pltpu.with_memory_space_constraint(a, pltpu.HBM) for a in
        (tile_columns, tile_count, grp_idx, adjacency, x_current, deg, w_self, w_neigh, b2)], *pieces)


def solution(mesh):
    in_specs = (
        P(("dom", "grp"), None),
        P(("dom", "grp"), None),
        P(),
        P(),
        P(),
        P(("dom", "grp"), None),
        P(("dom", "grp")),
        P(("dom", "grp"), None, None),
        P(("dom", "grp")),
        P(("dom", "grp"), None),
    )
    out_specs = P(("dom", "grp"), None)
    return jax.shard_map(
        on_device, mesh=mesh, in_specs=in_specs, out_specs=out_specs, check_vma=False
    )
```

```python
import functools

import jax
import jax.numpy as jnp
from jax import lax
from jax.experimental import pallas as pl
from jax.experimental.pallas import tpu as pltpu
from jax.sharding import PartitionSpec as P

CHUNK = 8


def _bits_kernel(counts_ref, adj_ref, out_ref, words_ref, mexp_ref, *, per_tile, tile):
    r = pl.program_id(0)
    count = counts_ref[r]
    kk = tile // 8

    @pl.when(r == 0)
    def _():
        rows = lax.broadcasted_iota(jnp.int32, (tile, 8 * tile), 0)
        cols = lax.broadcasted_iota(jnp.int32, (tile, 8 * tile), 1)
        jj = cols % tile
        hit = rows == (tile // 8) * (cols // tile) + jj // 8
        scale = lax.shift_left(jnp.ones_like(jj), 7 - jj % 8).astype(jnp.float32)
        mexp_ref[...] = jnp.where(hit, scale, 0.0).astype(jnp.bfloat16)

    for k in range(kk):
        words_ref[pl.ds(k * per_tile, per_tile), :] = adj_ref[0, :, pl.ds(k * tile, tile)]

    for c in range(per_tile // CHUNK):
        @pl.when(c * CHUNK < count)
        def _():
            words = jnp.concatenate(
                [words_ref[pl.ds(c * CHUNK + tl, kk, stride=per_tile), :] for tl in range(CHUNK)],
                axis=0)
            spread = jnp.dot(words.astype(jnp.bfloat16), mexp_ref[...],
                             preferred_element_type=jnp.float32)
            bits = (spread.astype(jnp.int32) & 128).astype(jnp.bfloat16)
            rows = []
            for s in range(8):
                rows.append(jnp.concatenate(
                    [bits[tl * kk:(tl + 1) * kk, s * tile:(s + 1) * tile] for tl in range(CHUNK)],
                    axis=1))
            out_ref[0, c] = jnp.concatenate(rows, axis=0)


def _layer_kernel(cols_ref, counts_ref, grp_ref, adj_ref, xc_ref, deg_ref, ws_ref, wn_ref, b_ref,
                  *rest, per_tile, tile, n_table, n_grp, dev_blocks):
    pieces = rest[:n_grp + 1]
    out_ref, table_ref, sems, acc_ref, perm_ref, pick_ref = rest[n_grp + 1:]
    r = pl.program_id(0)
    count = counts_ref[r]
    g = grp_ref[0]
    part = n_grp * dev_blocks

    @pl.when(r == 0)
    def _():
        ri = lax.broadcasted_iota(jnp.int32, (tile, tile), 0)
        ci = lax.broadcasted_iota(jnp.int32, (tile, tile), 1)
        kq = tile // 8
        perm_ref[...] = (ri == 8 * (ci % kq) + ci // kq).astype(jnp.bfloat16)
        pick_ref[...] = (ci == 8 * (ri % kq) + ri // kq).astype(jnp.float32)
        copies = []
        for d in range(n_grp):
            copies.append(pltpu.make_async_copy(
                pieces[d], table_ref.at[pl.ds(d * dev_blocks, dev_blocks)], sems.at[d]))
        n_halo = n_table - part
        copies.append(pltpu.make_async_copy(
            pieces[n_grp], table_ref.at[pl.ds(part, n_halo)], sems.at[n_grp]))
        for cp in copies:
            cp.start()
        for cp in copies:
            cp.wait()

    acc_ref[...] = jnp.zeros_like(acc_ref)

    def chunk(c, masked):
            a_cat = adj_ref[0, c]
            xs = []
            for tl in range(CHUNK):
                t = c * CHUNK + tl
                col = cols_ref[r, t]
                if n_grp == 4:
                    slot = jnp.bitwise_xor(col // dev_blocks, g)
                else:
                    slot = (g - col // dev_blocks + n_grp) % n_grp
                rel = slot * dev_blocks + col % dev_blocks
                col = jnp.clip(jnp.where(col < part, rel, col), 0, n_table - 1)
                xt = table_ref[col]
                if masked:
                    xt = jnp.where(t < count, xt, jnp.zeros_like(xt))
                xs.append(xt)
            x_cat = jnp.concatenate(xs, axis=0)
            acc_ref[...] += jnp.dot(a_cat, x_cat, preferred_element_type=jnp.float32)

    for c in range(per_tile // CHUNK):
        pl.when((c + 1) * CHUNK <= count)(functools.partial(chunk, c, False))
        pl.when((c * CHUNK < count) & (count < (c + 1) * CHUNK))(functools.partial(chunk, c, True))

    acc = acc_ref[...]
    totals = acc * (1.0 / 128.0)
    deg_row = deg_ref[pl.ds(r, 1), :].astype(jnp.float32)
    deg_perm = jnp.sum(pick_ref[...] * deg_row, axis=1, keepdims=True)
    avg_perm = (totals / deg_perm).astype(jnp.bfloat16)
    avg = jnp.dot(perm_ref[...], avg_perm, preferred_element_type=jnp.float32).astype(jnp.bfloat16)
    summed = (jnp.dot(xc_ref[...], ws_ref[...], preferred_element_type=jnp.float32)
              + jnp.dot(avg, wn_ref[...], preferred_element_type=jnp.float32) + b_ref[...])
    out_ref[...] = jnp.maximum(summed, 0.0).astype(out_ref.dtype)


def on_device(
    x_current,
    x_cached,
    w_self,
    w_neigh,
    bias,
    tile_columns,
    tile_count,
    adjacency,
    degree,
    boundary_blocks,
):
    node_rows, width = x_current.shape
    row_blocks, per_tile = tile_columns.shape
    tile_rows = node_rows // row_blocks
    hidden = w_self.shape[1]
    kk = tile_rows // 8
    assert per_tile % CHUNK == 0
    n_grp = lax.psum(1, "grp")
    chosen = x_cached.reshape(row_blocks, tile_rows, width)[boundary_blocks[0]]
    n_dom = lax.psum(1, "dom")
    n_dev = n_dom * n_grp
    spread_out = jnp.broadcast_to(chosen[None], (n_dev,) + chosen.shape).reshape(
        (n_dev * chosen.shape[0],) + chosen.shape[1:])
    halo_blocks = lax.all_to_all(spread_out, ("dom", "grp"), 0, 0, tiled=True)
    n_chunk = per_tile // CHUNK
    bits_call = pl.pallas_call(
        functools.partial(_bits_kernel, per_tile=per_tile, tile=tile_rows),
        grid_spec=pltpu.PrefetchScalarGridSpec(
            num_scalar_prefetch=1,
            grid=(row_blocks,),
            in_specs=[pl.BlockSpec((1, per_tile, tile_rows * kk), lambda r, *_: (r, 0, 0))],
            out_specs=pl.BlockSpec((1, n_chunk, tile_rows, CHUNK * tile_rows),
                                   lambda r, *_: (r, 0, 0, 0)),
            scratch_shapes=[pltpu.VMEM((per_tile * kk, tile_rows), jnp.int32),
                            pltpu.VMEM((tile_rows, 8 * tile_rows), jnp.bfloat16)],
        ),
        out_shape=jax.ShapeDtypeStruct((row_blocks, n_chunk, tile_rows, CHUNK * tile_rows),
                                       jnp.bfloat16),
        compiler_params=pltpu.CompilerParams(
            dimension_semantics=("arbitrary",), vmem_limit_bytes=32 * 1024 * 1024),
    )
    abits = bits_call(tile_count, adjacency)
    own_blocks = x_current.reshape(row_blocks, tile_rows, width)
    pieces = [own_blocks]
    if n_grp == 4:
        near = lax.ppermute(own_blocks, "grp", [(i, i ^ 1) for i in range(4)])
        far = lax.ppermute(own_blocks, "grp", [(i, i ^ 2) for i in range(4)])
        far, abits = lax.optimization_barrier((far, abits))
        far_near = lax.ppermute(far, "grp", [(i, i ^ 1) for i in range(4)])
        pieces += [near, far, far_near]
    else:
        for d in range(1, n_grp):
            pieces.append(lax.ppermute(own_blocks, "grp", [(i, (i + d) % n_grp) for i in range(n_grp)]))
    pieces.append(halo_blocks)
    n_table = n_grp * row_blocks + halo_blocks.shape[0]
    grp_idx = jnp.stack([lax.axis_index("grp"), lax.axis_index("grp")]).astype(jnp.int32)

    deg = degree.reshape(row_blocks, tile_rows)
    b2 = bias.reshape(1, hidden)


    kernel = functools.partial(_layer_kernel, per_tile=per_tile, tile=tile_rows, n_table=n_table,
                               n_grp=n_grp, dev_blocks=row_blocks)
    grid_spec = pltpu.PrefetchScalarGridSpec(
        num_scalar_prefetch=3,
        grid=(row_blocks,),
        in_specs=[
            pl.BlockSpec((1, n_chunk, tile_rows, CHUNK * tile_rows), lambda r, *_: (r, 0, 0, 0)),
            pl.BlockSpec((tile_rows, width), lambda r, *_: (r, 0)),
            pl.BlockSpec((row_blocks, tile_rows), lambda r, *_: (0, 0)),
            pl.BlockSpec((width, hidden), lambda r, *_: (0, 0)),
            pl.BlockSpec((width, hidden), lambda r, *_: (0, 0)),
            pl.BlockSpec((1, hidden), lambda r, *_: (0, 0)),
        ] + [pl.BlockSpec(memory_space=pl.ANY)] * (n_grp + 1),
        out_specs=pl.BlockSpec((tile_rows, hidden), lambda r, *_: (r, 0)),
        scratch_shapes=[pltpu.VMEM((n_table, tile_rows, width), jnp.bfloat16),
                        pltpu.SemaphoreType.DMA((n_grp + 1,)),
                        pltpu.VMEM((tile_rows, width), jnp.float32),
                        pltpu.VMEM((tile_rows, tile_rows), jnp.bfloat16),
                        pltpu.VMEM((tile_rows, tile_rows), jnp.float32)],
    )
    return pl.pallas_call(
        kernel,
        grid_spec=grid_spec,
        out_shape=jax.ShapeDtypeStruct((node_rows, hidden), jnp.bfloat16),
        compiler_params=pltpu.CompilerParams(
            dimension_semantics=("arbitrary",), vmem_limit_bytes=48 * 1024 * 1024),
    )(*[pltpu.with_memory_space_constraint(a, pltpu.HBM) for a in
        (tile_columns, tile_count, grp_idx, abits, x_current, deg, w_self, w_neigh, b2)], *pieces)


def solution(mesh):
    in_specs = (
        P(("dom", "grp"), None),
        P(("dom", "grp"), None),
        P(),
        P(),
        P(),
        P(("dom", "grp"), None),
        P(("dom", "grp")),
        P(("dom", "grp"), None, None),
        P(("dom", "grp")),
        P(("dom", "grp"), None),
    )
    out_specs = P(("dom", "grp"), None)
    return jax.shard_map(
        on_device, mesh=mesh, in_specs=in_specs, out_specs=out_specs, check_vma=False
    )
```

```python
import functools

import jax
import jax.numpy as jnp
from jax import lax
from jax.experimental import pallas as pl
from jax.experimental.pallas import tpu as pltpu
from jax.sharding import PartitionSpec as P

CHUNK = 4


def _expand_matrix(tile, dtype):
    words = tile // 8
    lanes = tile
    rows = lax.broadcasted_iota(jnp.int32, (lanes, 8 * tile), 0)
    cols = lax.broadcasted_iota(jnp.int32, (lanes, 8 * tile), 1)
    s = cols // tile
    j = cols % tile
    hit = rows == words * s + j // 8
    scale = lax.shift_left(jnp.int32(1), 7 - j % 8).astype(jnp.float32)
    return jnp.where(hit, scale, 0.0).astype(dtype)


def _perm_matrix(tile, dtype):
    kk = tile // 8
    rows = lax.broadcasted_iota(jnp.int32, (tile, tile), 0)
    cols = lax.broadcasted_iota(jnp.int32, (tile, tile), 1)
    return (rows == 8 * (cols % kk) + cols // kk).astype(dtype)


def _layer_kernel(cols_ref, counts_ref, grp_ref, adj_ref, xc_ref, deg_ref, w_ref, b_ref,
                  mexp_ref, perm_ref, *rest, per_tile, tile, n_table, n_grp, dev_blocks,
                  levels, per_dev):
    pieces = rest[:n_grp + 1]
    out_ref, table_ref, sems, words_ref, acc_ref = rest[n_grp + 1:]
    r = pl.program_id(0)
    count = counts_ref[r]
    g = grp_ref[0]
    me = grp_ref[1]
    part = n_grp * dev_blocks

    @pl.when(r == 0)
    def _():
        copies = []
        for d in range(n_grp):
            copies.append(pltpu.make_async_copy(
                pieces[d], table_ref.at[pl.ds(d * dev_blocks, dev_blocks)], sems.at[d]))
        n_halo = n_table - part
        copies.append(pltpu.make_async_copy(
            pieces[n_grp], table_ref.at[pl.ds(part, n_halo)], sems.at[n_grp]))
        for cp in copies:
            cp.start()
        for cp in copies:
            cp.wait()

    kk = tile // 8
    for k in range(kk):
        words_ref[pl.ds(k * per_tile, per_tile), :] = adj_ref[0, :, pl.ds(k * tile, tile)]
    acc_ref[...] = jnp.zeros_like(acc_ref)

    for c in range(per_tile // CHUNK):
        @pl.when(c * CHUNK < count)
        def _():
            words = jnp.concatenate(
                [words_ref[pl.ds(c * CHUNK + tl, kk, stride=per_tile), :] for tl in range(CHUNK)],
                axis=0)
            spread = jnp.dot(words.astype(jnp.bfloat16), mexp_ref[...],
                             preferred_element_type=jnp.float32)
            bits = (spread.astype(jnp.int32) & 128).astype(jnp.bfloat16)
            rows = []
            for s in range(8):
                rows.append(jnp.concatenate(
                    [bits[tl * kk:(tl + 1) * kk, s * tile:(s + 1) * tile] for tl in range(CHUNK)],
                    axis=1))
            a_cat = jnp.concatenate(rows, axis=0)
            xs = []
            for tl in range(CHUNK):
                t = c * CHUNK + tl
                col = cols_ref[r, t]
                if n_grp == 4:
                    slot = jnp.bitwise_xor(col // dev_blocks, g)
                else:
                    slot = (g - col // dev_blocks + n_grp) % n_grp
                rel = slot * dev_blocks + col % dev_blocks
                h = jnp.maximum(col - part, 0)
                x = jnp.bitwise_xor(h // per_dev, me)
                pos = jnp.int32(0)
                for bit in range(levels):
                    pos = pos + ((x >> bit) & 1) * (1 << (levels - 1 - bit))
                hrel = part + pos * per_dev + h % per_dev
                col = jnp.clip(jnp.where(col < part, rel, hrel), 0, n_table - 1)
                xt = table_ref[col]
                xs.append(jnp.where(t < count, xt, jnp.zeros_like(xt)))
            x_cat = jnp.concatenate(xs, axis=0)
            acc_ref[...] += jnp.dot(a_cat, x_cat, preferred_element_type=jnp.float32)

    acc = acc_ref[...]
    totals = acc * (1.0 / 128.0)
    deg_row = deg_ref[pl.ds(r, 1), :].astype(jnp.float32)
    pick = perm_ref[...].T > 0
    deg_perm = jnp.sum(jnp.where(pick, deg_row, 0.0), axis=1, keepdims=True)
    avg_perm = (totals / deg_perm).astype(jnp.bfloat16)
    avg = jnp.dot(perm_ref[...], avg_perm, preferred_element_type=jnp.float32).astype(jnp.bfloat16)
    lhs = jnp.concatenate([xc_ref[...], avg], axis=1)
    summed = jnp.dot(lhs, w_ref[...], preferred_element_type=jnp.float32) + b_ref[...]
    out_ref[...] = jnp.maximum(summed, 0.0).astype(out_ref.dtype)


def on_device(
    x_current,
    x_cached,
    w_self,
    w_neigh,
    bias,
    tile_columns,
    tile_count,
    adjacency,
    degree,
    boundary_blocks,
):
    node_rows, width = x_current.shape
    row_blocks, per_tile = tile_columns.shape
    tile_rows = node_rows // row_blocks
    hidden = w_self.shape[1]
    kk = tile_rows // 8
    assert per_tile % CHUNK == 0
    n_grp = lax.psum(1, "grp")
    chosen = x_cached.reshape(row_blocks, tile_rows, width)[boundary_blocks[0]]
    n_dom = lax.psum(1, "dom")
    n_dev = n_dom * n_grp
    levels = n_dev.bit_length() - 1
    assert 1 << levels == n_dev
    me = lax.axis_index("dom") * n_grp + lax.axis_index("grp")
    halo_blocks = chosen
    for lv in range(levels):
        mask = n_dev >> (lv + 1)
        theirs = lax.ppermute(halo_blocks, ("dom", "grp"), [(i, i ^ mask) for i in range(n_dev)])
        halo_blocks = jnp.concatenate([halo_blocks, theirs], axis=0)
    own_blocks = x_current.reshape(row_blocks, tile_rows, width)
    pieces = [own_blocks]
    if n_grp == 4:
        near = lax.ppermute(own_blocks, "grp", [(i, i ^ 1) for i in range(4)])
        far = lax.ppermute(own_blocks, "grp", [(i, i ^ 2) for i in range(4)])
        far_near = lax.ppermute(far, "grp", [(i, i ^ 1) for i in range(4)])
        pieces += [near, far, far_near]
    else:
        for d in range(1, n_grp):
            pieces.append(lax.ppermute(own_blocks, "grp", [(i, (i + d) % n_grp) for i in range(n_grp)]))
    pieces.append(halo_blocks)
    n_table = n_grp * row_blocks + halo_blocks.shape[0]
    grp_idx = jnp.stack([lax.axis_index("grp"), me]).astype(jnp.int32)

    deg = degree.reshape(row_blocks, tile_rows)
    w_cat = jnp.concatenate([w_self, w_neigh], axis=0)
    b2 = bias.reshape(1, hidden)
    mexp = _expand_matrix(tile_rows, jnp.bfloat16)
    perm = _perm_matrix(tile_rows, jnp.bfloat16)

    kernel = functools.partial(_layer_kernel, per_tile=per_tile, tile=tile_rows, n_table=n_table,
                               n_grp=n_grp, dev_blocks=row_blocks, levels=levels,
                               per_dev=chosen.shape[0])
    grid_spec = pltpu.PrefetchScalarGridSpec(
        num_scalar_prefetch=3,
        grid=(row_blocks,),
        in_specs=[
            pl.BlockSpec((1, per_tile, tile_rows * kk), lambda r, *_: (r, 0, 0)),
            pl.BlockSpec((tile_rows, width), lambda r, *_: (r, 0)),
            pl.BlockSpec((row_blocks, tile_rows), lambda r, *_: (0, 0)),
            pl.BlockSpec((2 * width, hidden), lambda r, *_: (0, 0)),
            pl.BlockSpec((1, hidden), lambda r, *_: (0, 0)),
            pl.BlockSpec((tile_rows, 8 * tile_rows), lambda r, *_: (0, 0)),
            pl.BlockSpec((tile_rows, tile_rows), lambda r, *_: (0, 0)),
        ] + [pl.BlockSpec(memory_space=pl.ANY)] * (n_grp + 1),
        out_specs=pl.BlockSpec((tile_rows, hidden), lambda r, *_: (r, 0)),
        scratch_shapes=[pltpu.VMEM((n_table, tile_rows, width), jnp.bfloat16),
                        pltpu.SemaphoreType.DMA((n_grp + 1,)),
                        pltpu.VMEM((per_tile * kk, tile_rows), jnp.int32),
                        pltpu.VMEM((tile_rows, width), jnp.float32)],
    )
    return pl.pallas_call(
        kernel,
        grid_spec=grid_spec,
        out_shape=jax.ShapeDtypeStruct((node_rows, hidden), jnp.bfloat16),
        compiler_params=pltpu.CompilerParams(
            dimension_semantics=("arbitrary",), vmem_limit_bytes=48 * 1024 * 1024),
    )(tile_columns, tile_count, grp_idx, adjacency, x_current, deg, w_cat, b2, mexp, perm, *pieces)


def solution(mesh):
    in_specs = (
        P(("dom", "grp"), None),
        P(("dom", "grp"), None),
        P(),
        P(),
        P(),
        P(("dom", "grp"), None),
        P(("dom", "grp")),
        P(("dom", "grp"), None, None),
        P(("dom", "grp")),
        P(("dom", "grp"), None),
    )
    out_specs = P(("dom", "grp"), None)
    return jax.shard_map(
        on_device, mesh=mesh, in_specs=in_specs, out_specs=out_specs, check_vma=False
    )
```

```python
import functools

import jax
import jax.numpy as jnp
from jax import lax
from jax.experimental import pallas as pl
from jax.experimental.pallas import tpu as pltpu
from jax.sharding import PartitionSpec as P

CHUNK = 8
RB = 2


def _layer_kernel(cols_ref, counts_ref, grp_ref, adj_ref, xc_ref, deg_ref, ws_ref, wn_ref, b_ref,
                  *rest, per_tile, tile, n_table, n_grp, dev_blocks,
                  levels, per_dev):
    pieces = rest[:n_grp + 1]
    out_ref, table_ref, sems, words_ref, acc_ref, mexp_ref, perm_ref, pick_ref = rest[n_grp + 1:]
    pid = pl.program_id(0)
    g = grp_ref[0]
    me = grp_ref[1]
    part = n_grp * dev_blocks

    @pl.when(pid == 0)
    def _():
        rows = lax.broadcasted_iota(jnp.int32, (tile, 8 * tile), 0)
        cols = lax.broadcasted_iota(jnp.int32, (tile, 8 * tile), 1)
        jj = cols % tile
        hit = rows == (tile // 8) * (cols // tile) + jj // 8
        scale = lax.shift_left(jnp.ones_like(jj), 7 - jj % 8).astype(jnp.float32)
        mexp_ref[...] = jnp.where(hit, scale, 0.0).astype(jnp.bfloat16)
        ri = lax.broadcasted_iota(jnp.int32, (tile, tile), 0)
        ci = lax.broadcasted_iota(jnp.int32, (tile, tile), 1)
        kq = tile // 8
        perm_ref[...] = (ri == 8 * (ci % kq) + ci // kq).astype(jnp.bfloat16)
        pick_ref[...] = (ci == 8 * (ri % kq) + ri // kq).astype(jnp.float32)
        copies = []
        for d in range(n_grp):
            copies.append(pltpu.make_async_copy(
                pieces[d], table_ref.at[pl.ds(d * dev_blocks, dev_blocks)], sems.at[d]))
        n_halo = n_table - part
        copies.append(pltpu.make_async_copy(
            pieces[n_grp], table_ref.at[pl.ds(part, n_halo)], sems.at[n_grp]))
        for cp in copies:
            cp.start()
        for cp in copies:
            cp.wait()

    def one_block(rb):
        r = pid * RB + rb
        count = counts_ref[r]
        kk = tile // 8
        for k in range(kk):
            words_ref[pl.ds(k * per_tile, per_tile), :] = adj_ref[rb, :, pl.ds(k * tile, tile)]
        acc_ref[...] = jnp.zeros_like(acc_ref)

        def chunk(c, masked):
                words = jnp.concatenate(
                    [words_ref[pl.ds(c * CHUNK + tl, kk, stride=per_tile), :] for tl in range(CHUNK)],
                    axis=0)
                spread = jnp.dot(words.astype(jnp.bfloat16), mexp_ref[...],
                                 preferred_element_type=jnp.float32)
                bits = (spread.astype(jnp.int32) & 128).astype(jnp.bfloat16)
                rows = []
                for s in range(8):
                    rows.append(jnp.concatenate(
                        [bits[tl * kk:(tl + 1) * kk, s * tile:(s + 1) * tile] for tl in range(CHUNK)],
                        axis=1))
                a_cat = jnp.concatenate(rows, axis=0)
                xs = []
                for tl in range(CHUNK):
                    t = c * CHUNK + tl
                    col = cols_ref[r, t]
                    if n_grp == 4:
                        slot = jnp.bitwise_xor(col // dev_blocks, g)
                    else:
                        slot = (g - col // dev_blocks + n_grp) % n_grp
                    rel = slot * dev_blocks + col % dev_blocks
                    h = jnp.maximum(col - part, 0)
                    x = jnp.bitwise_xor(h // per_dev, me)
                    pos = jnp.int32(0)
                    for bit in range(levels):
                        pos = pos + ((x >> bit) & 1) * (1 << (levels - 1 - bit))
                    hrel = part + pos * per_dev + h % per_dev
                    col = jnp.clip(jnp.where(col < part, rel, hrel), 0, n_table - 1)
                    xt = table_ref[col]
                    if masked:
                        xt = jnp.where(t < count, xt, jnp.zeros_like(xt))
                    xs.append(xt)
                x_cat = jnp.concatenate(xs, axis=0)
                acc_ref[...] += jnp.dot(a_cat, x_cat, preferred_element_type=jnp.float32)

        for c in range(per_tile // CHUNK):
            pl.when((c + 1) * CHUNK <= count)(functools.partial(chunk, c, False))
            pl.when((c * CHUNK < count) & (count < (c + 1) * CHUNK))(functools.partial(chunk, c, True))

        acc = acc_ref[...]
        totals = acc * (1.0 / 128.0)
        deg_row = deg_ref[pl.ds(r, 1), :].astype(jnp.float32)
        deg_perm = jnp.sum(pick_ref[...] * deg_row, axis=1, keepdims=True)
        avg_perm = (totals / deg_perm).astype(jnp.bfloat16)
        avg = jnp.dot(perm_ref[...], avg_perm, preferred_element_type=jnp.float32).astype(jnp.bfloat16)
        summed = (jnp.dot(xc_ref[pl.ds(rb * tile, tile), :], ws_ref[...], preferred_element_type=jnp.float32)
                  + jnp.dot(avg, wn_ref[...], preferred_element_type=jnp.float32) + b_ref[...])
        out_ref[pl.ds(rb * tile, tile), :] = jnp.maximum(summed, 0.0).astype(out_ref.dtype)

    for rb in range(RB):
        one_block(rb)


def on_device(
    x_current,
    x_cached,
    w_self,
    w_neigh,
    bias,
    tile_columns,
    tile_count,
    adjacency,
    degree,
    boundary_blocks,
):
    node_rows, width = x_current.shape
    row_blocks, per_tile = tile_columns.shape
    tile_rows = node_rows // row_blocks
    hidden = w_self.shape[1]
    kk = tile_rows // 8
    assert per_tile % CHUNK == 0 and row_blocks % RB == 0
    n_grp = lax.psum(1, "grp")
    chosen = x_cached.reshape(row_blocks, tile_rows, width)[boundary_blocks[0]]
    n_dom = lax.psum(1, "dom")
    n_dev = n_dom * n_grp
    levels = n_dev.bit_length() - 1
    assert 1 << levels == n_dev
    me = lax.axis_index("dom") * n_grp + lax.axis_index("grp")
    halo_blocks = chosen
    for lv in range(levels):
        mask = n_dev >> (lv + 1)
        theirs = lax.ppermute(halo_blocks, ("dom", "grp"), [(i, i ^ mask) for i in range(n_dev)])
        halo_blocks = jnp.concatenate([halo_blocks, theirs], axis=0)
    own_blocks = x_current.reshape(row_blocks, tile_rows, width)
    pieces = [own_blocks]
    if n_grp == 4:
        near = lax.ppermute(own_blocks, "grp", [(i, i ^ 1) for i in range(4)])
        far = lax.ppermute(own_blocks, "grp", [(i, i ^ 2) for i in range(4)])
        far_near = lax.ppermute(far, "grp", [(i, i ^ 1) for i in range(4)])
        pieces += [near, far, far_near]
    else:
        for d in range(1, n_grp):
            pieces.append(lax.ppermute(own_blocks, "grp", [(i, (i + d) % n_grp) for i in range(n_grp)]))
    pieces.append(halo_blocks)
    n_table = n_grp * row_blocks + halo_blocks.shape[0]
    grp_idx = jnp.stack([lax.axis_index("grp"), me]).astype(jnp.int32)

    deg = degree.reshape(row_blocks, tile_rows)
    b2 = bias.reshape(1, hidden)

    kernel = functools.partial(_layer_kernel, per_tile=per_tile, tile=tile_rows, n_table=n_table,
                               n_grp=n_grp, dev_blocks=row_blocks, levels=levels,
                               per_dev=chosen.shape[0])
    grid_spec = pltpu.PrefetchScalarGridSpec(
        num_scalar_prefetch=3,
        grid=(row_blocks // RB,),
        in_specs=[
            pl.BlockSpec((RB, per_tile, tile_rows * kk), lambda r, *_: (r, 0, 0)),
            pl.BlockSpec((RB * tile_rows, width), lambda r, *_: (r, 0)),
            pl.BlockSpec((row_blocks, tile_rows), lambda r, *_: (0, 0)),
            pl.BlockSpec((width, hidden), lambda r, *_: (0, 0)),
            pl.BlockSpec((width, hidden), lambda r, *_: (0, 0)),
            pl.BlockSpec((1, hidden), lambda r, *_: (0, 0)),
        ] + [pl.BlockSpec(memory_space=pl.ANY)] * (n_grp + 1),
        out_specs=pl.BlockSpec((RB * tile_rows, hidden), lambda r, *_: (r, 0)),
        scratch_shapes=[pltpu.VMEM((n_table, tile_rows, width), jnp.bfloat16),
                        pltpu.SemaphoreType.DMA((n_grp + 1,)),
                        pltpu.VMEM((per_tile * kk, tile_rows), jnp.int32),
                        pltpu.VMEM((tile_rows, width), jnp.float32),
                        pltpu.VMEM((tile_rows, 8 * tile_rows), jnp.bfloat16),
                        pltpu.VMEM((tile_rows, tile_rows), jnp.bfloat16),
                        pltpu.VMEM((tile_rows, tile_rows), jnp.float32)],
    )
    return pl.pallas_call(
        kernel,
        grid_spec=grid_spec,
        out_shape=jax.ShapeDtypeStruct((node_rows, hidden), jnp.bfloat16),
        compiler_params=pltpu.CompilerParams(
            dimension_semantics=("arbitrary",), vmem_limit_bytes=48 * 1024 * 1024),
    )(*[pltpu.with_memory_space_constraint(a, pltpu.HBM) for a in
        (tile_columns, tile_count, grp_idx, adjacency, x_current, deg, w_self, w_neigh, b2)], *pieces)


def solution(mesh):
    in_specs = (
        P(("dom", "grp"), None),
        P(("dom", "grp"), None),
        P(),
        P(),
        P(),
        P(("dom", "grp"), None),
        P(("dom", "grp")),
        P(("dom", "grp"), None, None),
        P(("dom", "grp")),
        P(("dom", "grp"), None),
    )
    out_specs = P(("dom", "grp"), None)
    return jax.shard_map(
        on_device, mesh=mesh, in_specs=in_specs, out_specs=out_specs, check_vma=False
    )
```
